512 devices in a mesh: lon: 64 (over x, z_hi, y, core), lat: 8 (over z_lo).
Axes of the slice: x: 4, y: 4, z: 16 (z_hi: 2, z_lo: 8; z = z_hi * 8 + z_lo), core: 2. Of those that a mesh axis runs over, the one named last changes fastest.
Arguments:
- state: float32 [4, 25, 64, 8192], P(None, None, 'lat', 'lon'), may hold values from -6 to 6
- sea_mask: int32 [64, 8192], P('lat', 'lon'), may hold values 0 or 1
- levels: int32 [64, 8192], P('lat', 'lon'), may hold values from 1 to 25
Outputs:
- new_state: float32 [4, 25, 64, 8192], P(None, None, 'lat', 'lon')
The draws below stay inside these ranges and needn't reach their ends.
All inputs are finite; a program needn't handle non-finite values. No bound on the sum of `sea_mask` on one device may be relied on, other than what follows from the above.
Results may differ from the reference program's by a relative error of at most 0.00002.
Values sent between devices are 32-bit elements; how exact they have to be, the bound alone decides.
No kernel may reach another device: no remote copies, remote signals or barrier semaphores. Data moves between devices by JAX's collectives and lax.ppermute only.
A program may use at most 64 MiB of HBM per device.

```python
import jax
import jax.numpy as jnp
from jax import lax

LEVELS = 25
NX = 8192
NY = 64


def plant(result, own_key, low, high):
    spot = [jax.random.randint(jax.random.fold_in(own_key, axis), (), 0, length) for axis, length in enumerate(result.shape)]
    longest = result.shape.index(max(result.shape))
    neighbour = spot[:longest] + [(spot[longest] + 1) % result.shape[longest]] + spot[longest + 1:]
    return result.at[tuple(spot)].set(low).at[tuple(neighbour)].set(high)


def block_scale(own_key, extent, cuts, smallest, high):
    loudness, own = 1.0, jax.random.fold_in(own_key, 6)
    for dim, shards_of in cuts:
        steps = jnp.exp(jax.random.uniform(jax.random.fold_in(own, dim), (shards_of,), jnp.float32, smallest / len(cuts), high / len(cuts)))
        loudness = loudness * jnp.repeat(steps, extent[dim] // shards_of).reshape([-1 if axis == dim else 1 for axis in range(len(extent))])
    return loudness


def noise(own_key, dims, deviation, limit, split=(), held_as=jnp.bfloat16):
    gain = block_scale(own_key, dims, split, -0.22, 0.18) if split else 1.0
    values = jax.random.normal(own_key, dims, jnp.float32) * deviation * gain
    return jnp.minimum(jnp.maximum(values, -limit), limit).astype(held_as)


def setup_inputs(seed: int = 0) -> dict:
    streams_of = jax.random.split(jax.random.key(seed), 4)
    return {
        "state": noise(streams_of[0], (4, LEVELS, NY, NX), 1.0, 6.0, ((2, 8), (3, 64)), jnp.float32),
        "sea_mask": plant((jax.random.randint(streams_of[1], (NY, NX), 0, 5) < 4).astype(jnp.int32), jax.random.fold_in(streams_of[1], 1), 0, 1),
        "levels": plant(jax.random.randint(streams_of[2], (NY, NX), 1, LEVELS + 1), jax.random.fold_in(streams_of[2], 1), 1, LEVELS).astype(jnp.int32),
    }


TIME_INCREMENT = 0.1
SCALAR_MIXING = 0.4
VISCOSITY = 0.4
THERMAL = 0.2
HALINE = 0.8
GRAVITY = 0.1


def inner_region(field, row_shift, col_shift):
    n_rows = field.shape[-2]
    n_cols = field.shape[-1]
    return field[..., 2 + row_shift:n_rows - 2 + row_shift, 2 + col_shift:n_cols - 2 + col_shift]


def diff_lon(field):
    return (8.0 * (inner_region(field, 0, 1) - inner_region(field, 0, -1)) - (inner_region(field, 0, 2) - inner_region(field, 0, -2))) / 12.0


def diff_lat(field):
    return (8.0 * (inner_region(field, 1, 0) - inner_region(field, -1, 0)) - (inner_region(field, 2, 0) - inner_region(field, -2, 0))) / 12.0


def second_derivative_sum(field):
    return inner_region(field, 0, 1) + inner_region(field, 0, -1) + inner_region(field, 1, 0) + inner_region(field, -1, 0) - 4.0 * inner_region(field, 0, 0)


def coriolis(row_index, total):
    mirrored = jnp.where(row_index >= total, 2 * total - 1 - row_index, row_index)
    return (1.2 * jnp.sin(-1.3 + 2.8 * (mirrored.astype(jnp.float32) + 0.5) / total))[:, None]


def advance_solution(heat_content_level, saltiness_grid, eastward_flow, northward_flow, weight_of_column, sea_cells_count, earth_rotation_term):
    east = inner_region(eastward_flow, 0, 0)
    north = inner_region(northward_flow, 0, 0)

    def running_solution(field):
        return east * diff_lon(field) + north * diff_lat(field)

    next_heat_level = sea_cells_count * (inner_region(heat_content_level, 0, 0) + TIME_INCREMENT * (SCALAR_MIXING * second_derivative_sum(heat_content_level) - running_solution(heat_content_level)))
    next_saltiness = sea_cells_count * (inner_region(saltiness_grid, 0, 0) + TIME_INCREMENT * (SCALAR_MIXING * second_derivative_sum(saltiness_grid) - running_solution(saltiness_grid)))
    next_eastward_flow = sea_cells_count * (east + TIME_INCREMENT * (earth_rotation_term * north - diff_lon(weight_of_column) - running_solution(eastward_flow) + VISCOSITY * second_derivative_sum(eastward_flow)))
    next_northward_flow = sea_cells_count * (north + TIME_INCREMENT * (-earth_rotation_term * east - diff_lat(weight_of_column) - running_solution(northward_flow) + VISCOSITY * second_derivative_sum(northward_flow)))
    return jnp.stack([next_heat_level, next_saltiness, next_eastward_flow, next_northward_flow])


def fold_pad(state):
    lon_wide = jnp.concatenate([state[..., -2:], state, state[..., :2]], axis=-1)
    fold_signs = jnp.array([1.0, 1.0, -1.0, -1.0], dtype=state.dtype).reshape(4, 1, 1, 1)
    northern = jnp.flip(lon_wide[:, :, -2:, :], axis=(2, 3)) * fold_signs
    southern = jnp.zeros_like(lon_wide[:, :, :2, :])
    return jnp.concatenate([southern, lon_wide, northern], axis=2)


def reference(state, sea_mask, levels):
    depth_index = jnp.arange(LEVELS, dtype=jnp.int32)[:, None, None]
    sea_cells_count = ((sea_mask[None] == 1) & (depth_index < levels[None])).astype(state.dtype)
    earth_rotation_term = coriolis(jnp.arange(NY, dtype=jnp.int32), NY)
    for step in range(2):
        padded = fold_pad(state)
        weight_of_column = GRAVITY * jnp.cumsum(HALINE * padded[1] - THERMAL * padded[0], axis=0)

        def one_level(pieces):
            return advance_solution(pieces[0], pieces[1], pieces[2], pieces[3], pieces[4], pieces[5], earth_rotation_term)

        moved = lax.map(one_level, (padded[0], padded[1], padded[2], padded[3], weight_of_column, sea_cells_count))
        state = jnp.transpose(moved, (1, 0, 2, 3))
    return state
```

```python
import jax
import jax.numpy as jnp
from jax import lax
from jax.sharding import PartitionSpec as P

TIME_INCREMENT = 0.1
SCALAR_MIXING = 0.4
VISCOSITY = 0.4
THERMAL = 0.2
HALINE = 0.8
GRAVITY = 0.1
MARGIN = 2


def coriolis(row_index, total):
    mirrored = jnp.where(row_index >= total, 2 * total - 1 - row_index, row_index)
    return (1.2 * jnp.sin(-1.3 + 2.8 * (mirrored.astype(jnp.float32) + 0.5) / total))[:, None]


def exchange(x, fold_signs):
    n_lon = lax.axis_size("lon")
    n_lat = lax.axis_size("lat")
    east_ward = [(i, (i + 1) % n_lon) for i in range(n_lon)]
    west_ward = [(j, i) for i, j in east_ward]
    west = lax.ppermute(x[..., -MARGIN:], "lon", east_ward)
    east = lax.ppermute(x[..., :MARGIN], "lon", west_ward)
    north_ward = [(i, i + 1) for i in range(n_lat - 1)]
    south_ward = [(j, i) for i, j in north_ward]
    south = lax.ppermute(x[:, :, -MARGIN:, :], "lat", north_ward)
    north = lax.ppermute(x[:, :, :MARGIN, :], "lat", south_ward)
    top = n_lat - 1
    pairs = [(l * n_lat + top, (n_lon - 1 - l) * n_lat + top) for l in range(n_lon)]
    mirror = lax.ppermute(x[:, :, -MARGIN:, :], ("lon", "lat"), pairs)
    folded = jnp.flip(mirror, axis=(2, 3)) * fold_signs
    north = jnp.where(lax.axis_index("lat") == n_lat - 1, folded, north)
    return west, east, south, north


def step(x, wet, cor, fold_signs):
    rows_n, cols_n = x.shape[2], x.shape[3]
    west, east, south, north = exchange(x, fold_signs)
    rows = jnp.concatenate([south, x, north], axis=2)
    cols = jnp.concatenate([west, x, east], axis=3)

    def at_col(f, s):
        return f[..., MARGIN + s : MARGIN + s + cols_n]

    def at_row(f, s):
        return f[..., MARGIN + s : MARGIN + s + rows_n, :]

    def dx(f):
        return (8.0 * (at_col(f, 1) - at_col(f, -1)) - (at_col(f, 2) - at_col(f, -2))) / 12.0

    def dy(f):
        return (8.0 * (at_row(f, 1) - at_row(f, -1)) - (at_row(f, 2) - at_row(f, -2))) / 12.0

    def lap(fc, fr, f):
        return at_col(fc, 1) + at_col(fc, -1) + at_row(fr, 1) + at_row(fr, -1) - 4.0 * f

    p_rows = GRAVITY * jnp.cumsum(HALINE * rows[1] - THERMAL * rows[0], axis=0)
    p_cols = GRAVITY * jnp.cumsum(HALINE * cols[1] - THERMAL * cols[0], axis=0)
    east_v, north_v = x[2], x[3]

    def adv(i):
        return east_v * dx(cols[i]) + north_v * dy(rows[i])

    heat = wet * (x[0] + TIME_INCREMENT * (SCALAR_MIXING * lap(cols[0], rows[0], x[0]) - adv(0)))
    salt = wet * (x[1] + TIME_INCREMENT * (SCALAR_MIXING * lap(cols[1], rows[1], x[1]) - adv(1)))
    u = wet * (
        east_v
        + TIME_INCREMENT
        * (cor * north_v - dx(p_cols) - adv(2) + VISCOSITY * lap(cols[2], rows[2], east_v))
    )
    v = wet * (
        north_v
        + TIME_INCREMENT
        * (-cor * east_v - dy(p_rows) - adv(3) + VISCOSITY * lap(cols[3], rows[3], north_v))
    )
    return jnp.stack([heat, salt, u, v])


def shards(state, sea_mask, levels):
    level_count = state.shape[1]
    tile_rows = state.shape[2]
    depth_index = jnp.arange(level_count, dtype=jnp.int32)[:, None, None]
    wet = ((sea_mask[None] == 1) & (depth_index < levels[None])).astype(jnp.float32)
    total = lax.axis_size("lat") * tile_rows
    own_rows = lax.axis_index("lat") * tile_rows + jnp.arange(tile_rows, dtype=jnp.int32)
    cor = coriolis(own_rows, total)
    fold_signs = jnp.array([1.0, 1.0, -1.0, -1.0], dtype=jnp.float32).reshape(4, 1, 1, 1)
    for _ in range(2):
        state = step(state, wet, cor, fold_signs)
    return state


def solution(mesh):
    return jax.shard_map(
        shards,
        mesh=mesh,
        in_specs=(P(None, None, "lat", "lon"), P("lat", "lon"), P("lat", "lon")),
        out_specs=P(None, None, "lat", "lon"),
        check_vma=False,
    )
```

```python
import jax
import jax.numpy as jnp
from jax import lax
from jax.sharding import PartitionSpec as P

TIME_INCREMENT = 0.1
SCALAR_MIXING = 0.4
VISCOSITY = 0.4
THERMAL = 0.2
HALINE = 0.8
GRAVITY = 0.1
MARGIN = 2


def coriolis(row_index, total):
    mirrored = jnp.where(row_index >= total, 2 * total - 1 - row_index, row_index)
    return (1.2 * jnp.sin(-1.3 + 2.8 * (mirrored.astype(jnp.float32) + 0.5) / total))[:, None]


def exchange(x, fold_signs):
    n_lon = lax.axis_size("lon")
    n_lat = lax.axis_size("lat")
    east_ward = [(i, (i + 1) % n_lon) for i in range(n_lon)]
    west_ward = [(j, i) for i, j in east_ward]
    west = lax.ppermute(x[..., -MARGIN:], "lon", east_ward)
    east = lax.ppermute(x[..., :MARGIN], "lon", west_ward)
    lat = lax.axis_index("lat")
    odd = lat % 2 == 1
    top_rows = x[:, :, -MARGIN:, :]
    bottom_rows = x[:, :, :MARGIN, :]
    to_odd = lax.ppermute(
        jnp.where(odd, bottom_rows, top_rows),
        ("lon", "lat"),
        [(l * n_lat + i, l * n_lat + (i ^ 1)) for l in range(n_lon) for i in range(n_lat)],
    )
    inner = [(i, i + 1) for i in range(1, n_lat - 1, 2)]
    inner = inner + [(j, i) for i, j in inner]
    top = n_lat - 1
    pairs = [(l * n_lat + i, l * n_lat + j) for l in range(n_lon) for i, j in inner]
    pairs = pairs + [(l * n_lat + top, (n_lon - 1 - l) * n_lat + top) for l in range(n_lon)]
    to_even = lax.ppermute(jnp.where(odd, top_rows, bottom_rows), ("lon", "lat"), pairs)
    folded = jnp.flip(to_even, axis=(2, 3)) * fold_signs
    north = jnp.where(odd, jnp.where(lat == top, folded, to_even), to_odd)
    south = jnp.where(odd, to_odd, to_even)
    return west, east, south, north


def step(x, wet, cor, fold_signs):
    rows_n, cols_n = x.shape[2], x.shape[3]
    west, east, south, north = exchange(x, fold_signs)
    rows = jnp.concatenate([south, x, north], axis=2)
    cols = jnp.concatenate([west, x, east], axis=3)

    def at_col(f, s):
        return f[..., MARGIN + s : MARGIN + s + cols_n]

    def at_row(f, s):
        return f[..., MARGIN + s : MARGIN + s + rows_n, :]

    def dx(f):
        return (8.0 * (at_col(f, 1) - at_col(f, -1)) - (at_col(f, 2) - at_col(f, -2))) / 12.0

    def dy(f):
        return (8.0 * (at_row(f, 1) - at_row(f, -1)) - (at_row(f, 2) - at_row(f, -2))) / 12.0

    def lap(fc, fr, f):
        return at_col(fc, 1) + at_col(fc, -1) + at_row(fr, 1) + at_row(fr, -1) - 4.0 * f

    p_rows = GRAVITY * jnp.cumsum(HALINE * rows[1] - THERMAL * rows[0], axis=0)
    p_cols = GRAVITY * jnp.cumsum(HALINE * cols[1] - THERMAL * cols[0], axis=0)
    east_v, north_v = x[2], x[3]

    def adv(i):
        return east_v * dx(cols[i]) + north_v * dy(rows[i])

    heat = wet * (x[0] + TIME_INCREMENT * (SCALAR_MIXING * lap(cols[0], rows[0], x[0]) - adv(0)))
    salt = wet * (x[1] + TIME_INCREMENT * (SCALAR_MIXING * lap(cols[1], rows[1], x[1]) - adv(1)))
    u = wet * (
        east_v
        + TIME_INCREMENT
        * (cor * north_v - dx(p_cols) - adv(2) + VISCOSITY * lap(cols[2], rows[2], east_v))
    )
    v = wet * (
        north_v
        + TIME_INCREMENT
        * (-cor * east_v - dy(p_rows) - adv(3) + VISCOSITY * lap(cols[3], rows[3], north_v))
    )
    return jnp.stack([heat, salt, u, v])


def shards(state, sea_mask, levels):
    level_count = state.shape[1]
    tile_rows = state.shape[2]
    depth_index = jnp.arange(level_count, dtype=jnp.int32)[:, None, None]
    wet = ((sea_mask[None] == 1) & (depth_index < levels[None])).astype(jnp.float32)
    total = lax.axis_size("lat") * tile_rows
    own_rows = lax.axis_index("lat") * tile_rows + jnp.arange(tile_rows, dtype=jnp.int32)
    cor = coriolis(own_rows, total)
    fold_signs = jnp.array([1.0, 1.0, -1.0, -1.0], dtype=jnp.float32).reshape(4, 1, 1, 1)
    for _ in range(2):
        state = step(state, wet, cor, fold_signs)
    return state


def solution(mesh):
    return jax.shard_map(
        shards,
        mesh=mesh,
        in_specs=(P(None, None, "lat", "lon"), P("lat", "lon"), P("lat", "lon")),
        out_specs=P(None, None, "lat", "lon"),
        check_vma=False,
    )
```

```python
import jax
import jax.numpy as jnp
from jax import lax
from jax.sharding import PartitionSpec as P

TIME_INCREMENT = 0.1
SCALAR_MIXING = 0.4
VISCOSITY = 0.4
THERMAL = 0.2
HALINE = 0.8
GRAVITY = 0.1
MARGIN = 2
WIDE = 2 * MARGIN


def coriolis(row_index, total):
    mirrored = jnp.where(row_index >= total, 2 * total - 1 - row_index, row_index)
    return (1.2 * jnp.sin(-1.3 + 2.8 * (mirrored.astype(jnp.float32) + 0.5) / total))[:, None]


def send(block, axes, pairs):
    moved = lax.ppermute(block.reshape(-1), axes, pairs)
    return moved.reshape(block.shape)


def gather_wide(x, signs):
    n_lon = lax.axis_size("lon")
    n_lat = lax.axis_size("lat")
    east_ward = [(i, (i + 1) % n_lon) for i in range(n_lon)]
    west_ward = [(j, i) for i, j in east_ward]
    west = send(x[..., -WIDE:], "lon", east_ward)
    east = send(x[..., :WIDE], "lon", west_ward)
    lon_wide = jnp.concatenate([west, x, east], axis=2)

    lat = lax.axis_index("lat")
    odd = lat % 2 == 1
    top_rows = lon_wide[:, -WIDE:, :]
    bottom_rows = lon_wide[:, :WIDE, :]
    to_odd = send(
        jnp.where(odd, bottom_rows, top_rows),
        ("lon", "lat"),
        [(l * n_lat + i, l * n_lat + (i ^ 1)) for l in range(n_lon) for i in range(n_lat)],
    )
    inner = [(i, i + 1) for i in range(1, n_lat - 1, 2)]
    inner = inner + [(j, i) for i, j in inner]
    top = n_lat - 1
    pairs = [(l * n_lat + i, l * n_lat + j) for l in range(n_lon) for i, j in inner]
    pairs = pairs + [(l * n_lat + top, (n_lon - 1 - l) * n_lat + top) for l in range(n_lon)]
    to_even = send(jnp.where(odd, top_rows, bottom_rows), ("lon", "lat"), pairs)
    folded = jnp.flip(to_even, axis=(1, 2)) * signs
    north = jnp.where(odd, jnp.where(lat == top, folded, to_even), to_odd)
    south = jnp.where(odd, to_odd, to_even)
    return jnp.concatenate([south, lon_wide, north], axis=1)


def advance(f, wet, cor):
    rows_n = f.shape[2] - 2 * MARGIN
    cols_n = f.shape[3] - 2 * MARGIN

    def at(g, dr, dc):
        return g[..., MARGIN + dr : MARGIN + dr + rows_n, MARGIN + dc : MARGIN + dc + cols_n]

    def dx(g):
        return (8.0 * (at(g, 0, 1) - at(g, 0, -1)) - (at(g, 0, 2) - at(g, 0, -2))) / 12.0

    def dy(g):
        return (8.0 * (at(g, 1, 0) - at(g, -1, 0)) - (at(g, 2, 0) - at(g, -2, 0))) / 12.0

    def lap(g):
        return at(g, 0, 1) + at(g, 0, -1) + at(g, 1, 0) + at(g, -1, 0) - 4.0 * at(g, 0, 0)

    pressure = GRAVITY * jnp.cumsum(HALINE * f[1] - THERMAL * f[0], axis=0)
    east_v, north_v = at(f[2], 0, 0), at(f[3], 0, 0)

    def adv(g):
        return east_v * dx(g) + north_v * dy(g)

    heat = wet * (at(f[0], 0, 0) + TIME_INCREMENT * (SCALAR_MIXING * lap(f[0]) - adv(f[0])))
    salt = wet * (at(f[1], 0, 0) + TIME_INCREMENT * (SCALAR_MIXING * lap(f[1]) - adv(f[1])))
    u = wet * (
        east_v
        + TIME_INCREMENT * (cor * north_v - dx(pressure) - adv(f[2]) + VISCOSITY * lap(f[2]))
    )
    v = wet * (
        north_v
        + TIME_INCREMENT * (-cor * east_v - dy(pressure) - adv(f[3]) + VISCOSITY * lap(f[3]))
    )
    return jnp.stack([heat, salt, u, v])


def shards(state, sea_mask, levels):
    n_fields, level_count, tile_rows, tile_cols = state.shape
    depth_index = jnp.arange(level_count, dtype=jnp.int32)[:, None, None]
    depth = jnp.where(sea_mask == 1, levels, 0).astype(jnp.float32)
    channels = jnp.concatenate([state.reshape(n_fields * level_count, tile_rows, tile_cols), depth[None]])
    signs = jnp.array([1.0, 1.0, -1.0, -1.0], dtype=jnp.float32)
    signs = jnp.concatenate([jnp.repeat(signs, level_count), jnp.ones((1,), jnp.float32)])
    wide = gather_wide(channels, signs[:, None, None])

    lat = lax.axis_index("lat")
    total = lax.axis_size("lat") * tile_rows
    first_row = lat * tile_rows

    grown = wide[:, MARGIN:-MARGIN, MARGIN:-MARGIN]
    grown_depth = grown[-1]
    grown_wet = (depth_index < grown_depth[None]).astype(jnp.float32)
    grown_rows = first_row - MARGIN + jnp.arange(tile_rows + 2 * MARGIN, dtype=jnp.int32)
    fields = wide[:-1].reshape(n_fields, level_count, *wide.shape[1:])
    once = advance(fields, grown_wet, coriolis(grown_rows, total))
    south_edge = (lat == 0) & (grown_rows < 0)
    once = jnp.where(south_edge[:, None], 0.0, once)

    wet = (depth_index < depth[None]).astype(jnp.float32)
    own_rows = first_row + jnp.arange(tile_rows, dtype=jnp.int32)
    return advance(once, wet, coriolis(own_rows, total))


def solution(mesh):
    return jax.shard_map(
        shards,
        mesh=mesh,
        in_specs=(P(None, None, "lat", "lon"), P("lat", "lon"), P("lat", "lon")),
        out_specs=P(None, None, "lat", "lon"),
        check_vma=False,
    )
```

```python
import jax
import jax.numpy as jnp
from jax import lax
from jax.sharding import PartitionSpec as P

TIME_INCREMENT = 0.1
SCALAR_MIXING = 0.4
VISCOSITY = 0.4
THERMAL = 0.2
HALINE = 0.8
GRAVITY = 0.1
MARGIN = 2
WIDE = 2 * MARGIN


def coriolis(row_index, total):
    mirrored = jnp.where(row_index >= total, 2 * total - 1 - row_index, row_index)
    return (1.2 * jnp.sin(-1.3 + 2.8 * (mirrored.astype(jnp.float32) + 0.5) / total))[:, None]


def send(block, axes, pairs):
    moved = lax.ppermute(block.reshape(-1), axes, pairs)
    return moved.reshape(block.shape)


def gather_wide(x, signs):
    n_lon = lax.axis_size("lon")
    n_lat = lax.axis_size("lat")
    lon = lax.axis_index("lon")
    lon_odd = lon % 2 == 1
    east_cols = x[..., -WIDE:]
    west_cols = x[..., :WIDE]
    on_chip = send(
        jnp.where(lon_odd, west_cols, east_cols), "lon", [(m, m ^ 1) for m in range(n_lon)]
    )
    across = [(m, (m + 1) % n_lon) for m in range(1, n_lon, 2)]
    across = across + [(j, i) for i, j in across]
    off_chip = send(jnp.where(lon_odd, east_cols, west_cols), "lon", across)
    west = jnp.where(lon_odd, on_chip, off_chip)
    east = jnp.where(lon_odd, off_chip, on_chip)
    lon_wide = jnp.concatenate([west, x, east], axis=2)

    lat = lax.axis_index("lat")
    odd = lat % 2 == 1
    top_rows = lon_wide[:, -WIDE:, :]
    bottom_rows = lon_wide[:, :WIDE, :]
    to_odd = send(
        jnp.where(odd, bottom_rows, top_rows),
        ("lon", "lat"),
        [(l * n_lat + i, l * n_lat + (i ^ 1)) for l in range(n_lon) for i in range(n_lat)],
    )
    inner = [(i, i + 1) for i in range(1, n_lat - 1, 2)]
    inner = inner + [(j, i) for i, j in inner]
    top = n_lat - 1
    pairs = [(l * n_lat + i, l * n_lat + j) for l in range(n_lon) for i, j in inner]
    pairs = pairs + [(l * n_lat + top, (n_lon - 1 - l) * n_lat + top) for l in range(n_lon)]
    to_even = send(jnp.where(odd, top_rows, bottom_rows), ("lon", "lat"), pairs)
    folded = jnp.flip(to_even, axis=(1, 2)) * signs
    north = jnp.where(odd, jnp.where(lat == top, folded, to_even), to_odd)
    south = jnp.where(odd, to_odd, to_even)
    return jnp.concatenate([south, lon_wide, north], axis=1)


def advance(f, wet, cor):
    rows_n = f.shape[2] - 2 * MARGIN
    cols_n = f.shape[3] - 2 * MARGIN

    def at(g, dr, dc):
        return g[..., MARGIN + dr : MARGIN + dr + rows_n, MARGIN + dc : MARGIN + dc + cols_n]

    def dx(g):
        return (8.0 * (at(g, 0, 1) - at(g, 0, -1)) - (at(g, 0, 2) - at(g, 0, -2))) / 12.0

    def dy(g):
        return (8.0 * (at(g, 1, 0) - at(g, -1, 0)) - (at(g, 2, 0) - at(g, -2, 0))) / 12.0

    def lap(g):
        return at(g, 0, 1) + at(g, 0, -1) + at(g, 1, 0) + at(g, -1, 0) - 4.0 * at(g, 0, 0)

    pressure = GRAVITY * jnp.cumsum(HALINE * f[1] - THERMAL * f[0], axis=0)
    east_v, north_v = at(f[2], 0, 0), at(f[3], 0, 0)

    def adv(g):
        return east_v * dx(g) + north_v * dy(g)

    heat = wet * (at(f[0], 0, 0) + TIME_INCREMENT * (SCALAR_MIXING * lap(f[0]) - adv(f[0])))
    salt = wet * (at(f[1], 0, 0) + TIME_INCREMENT * (SCALAR_MIXING * lap(f[1]) - adv(f[1])))
    u = wet * (
        east_v
        + TIME_INCREMENT * (cor * north_v - dx(pressure) - adv(f[2]) + VISCOSITY * lap(f[2]))
    )
    v = wet * (
        north_v
        + TIME_INCREMENT * (-cor * east_v - dy(pressure) - adv(f[3]) + VISCOSITY * lap(f[3]))
    )
    return jnp.stack([heat, salt, u, v])


def shards(state, sea_mask, levels):
    n_fields, level_count, tile_rows, tile_cols = state.shape
    depth_index = jnp.arange(level_count, dtype=jnp.int32)[:, None, None]
    depth = jnp.where(sea_mask == 1, levels, 0).astype(jnp.float32)
    channels = jnp.concatenate([state.reshape(n_fields * level_count, tile_rows, tile_cols), depth[None]])
    signs = jnp.array([1.0, 1.0, -1.0, -1.0], dtype=jnp.float32)
    signs = jnp.concatenate([jnp.repeat(signs, level_count), jnp.ones((1,), jnp.float32)])
    wide = gather_wide(channels, signs[:, None, None])

    lat = lax.axis_index("lat")
    total = lax.axis_size("lat") * tile_rows
    first_row = lat * tile_rows

    grown = wide[:, MARGIN:-MARGIN, MARGIN:-MARGIN]
    grown_depth = grown[-1]
    grown_wet = (depth_index < grown_depth[None]).astype(jnp.float32)
    grown_rows = first_row - MARGIN + jnp.arange(tile_rows + 2 * MARGIN, dtype=jnp.int32)
    fields = wide[:-1].reshape(n_fields, level_count, *wide.shape[1:])
    once = advance(fields, grown_wet, coriolis(grown_rows, total))
    south_edge = (lat == 0) & (grown_rows < 0)
    once = jnp.where(south_edge[:, None], 0.0, once)

    wet = (depth_index < depth[None]).astype(jnp.float32)
    own_rows = first_row + jnp.arange(tile_rows, dtype=jnp.int32)
    return advance(once, wet, coriolis(own_rows, total))


def solution(mesh):
    return jax.shard_map(
        shards,
        mesh=mesh,
        in_specs=(P(None, None, "lat", "lon"), P("lat", "lon"), P("lat", "lon")),
        out_specs=P(None, None, "lat", "lon"),
        check_vma=False,
    )
```

```python
import jax
import jax.numpy as jnp
from jax import lax
from jax.sharding import PartitionSpec as P

TIME_INCREMENT = 0.1
SCALAR_MIXING = 0.4
VISCOSITY = 0.4
THERMAL = 0.2
HALINE = 0.8
GRAVITY = 0.1
MARGIN = 2
WIDE = 2 * MARGIN


def coriolis(row_index, total):
    mirrored = jnp.where(row_index >= total, 2 * total - 1 - row_index, row_index)
    return (1.2 * jnp.sin(-1.3 + 2.8 * (mirrored.astype(jnp.float32) + 0.5) / total))[:, None]


def gather_wide(x, signs):
    n_lon = lax.axis_size("lon")
    n_lat = lax.axis_size("lat")

    lat = lax.axis_index("lat")
    odd = lat % 2 == 1
    top_rows = x[:, -WIDE:, :]
    bottom_rows = x[:, :WIDE, :]
    inner = [(i, i + 1) for i in range(1, n_lat - 1, 2)]
    inner = inner + [(j, i) for i, j in inner]
    top = n_lat - 1
    pairs = [(l * n_lat + i, l * n_lat + j) for l in range(n_lon) for i, j in inner]
    pairs = pairs + [(l * n_lat + top, (n_lon - 1 - l) * n_lat + top) for l in range(n_lon)]
    to_even = lax.ppermute(jnp.where(odd, top_rows, bottom_rows), ("lon", "lat"), pairs)
    to_odd = lax.ppermute(
        jnp.where(odd, bottom_rows, top_rows),
        ("lon", "lat"),
        [(l * n_lat + i, l * n_lat + (i ^ 1)) for l in range(n_lon) for i in range(n_lat)],
    )
    folded = jnp.flip(to_even, axis=(1, 2)) * signs
    north = jnp.where(odd, jnp.where(lat == top, folded, to_even), to_odd)
    south = jnp.where(odd, to_odd, to_even)
    lat_wide = jnp.concatenate([south, x, north], axis=1)

    lon = lax.axis_index("lon")
    lon_odd = lon % 2 == 1
    edge_shape = lat_wide[..., :WIDE].shape
    east_cols = lat_wide[..., -WIDE:].reshape(-1)
    west_cols = lat_wide[..., :WIDE].reshape(-1)
    on_chip = lax.ppermute(
        jnp.where(lon_odd, west_cols, east_cols), "lon", [(m, m ^ 1) for m in range(n_lon)]
    )
    across = [(m, (m + 1) % n_lon) for m in range(1, n_lon, 2)]
    across = across + [(j, i) for i, j in across]
    off_chip = lax.ppermute(jnp.where(lon_odd, east_cols, west_cols), "lon", across)
    west = jnp.where(lon_odd, on_chip, off_chip).reshape(edge_shape)
    east = jnp.where(lon_odd, off_chip, on_chip).reshape(edge_shape)
    return jnp.concatenate([west, lat_wide, east], axis=2)


def advance(f, wet, cor):
    rows_n = f.shape[2] - 2 * MARGIN
    cols_n = f.shape[3] - 2 * MARGIN

    def at(g, dr, dc):
        return g[..., MARGIN + dr : MARGIN + dr + rows_n, MARGIN + dc : MARGIN + dc + cols_n]

    def dx(g):
        return (8.0 * (at(g, 0, 1) - at(g, 0, -1)) - (at(g, 0, 2) - at(g, 0, -2))) / 12.0

    def dy(g):
        return (8.0 * (at(g, 1, 0) - at(g, -1, 0)) - (at(g, 2, 0) - at(g, -2, 0))) / 12.0

    def lap(g):
        return at(g, 0, 1) + at(g, 0, -1) + at(g, 1, 0) + at(g, -1, 0) - 4.0 * at(g, 0, 0)

    pressure = GRAVITY * jnp.cumsum(HALINE * f[1] - THERMAL * f[0], axis=0)
    east_v, north_v = at(f[2], 0, 0), at(f[3], 0, 0)

    def adv(g):
        return east_v * dx(g) + north_v * dy(g)

    heat = wet * (at(f[0], 0, 0) + TIME_INCREMENT * (SCALAR_MIXING * lap(f[0]) - adv(f[0])))
    salt = wet * (at(f[1], 0, 0) + TIME_INCREMENT * (SCALAR_MIXING * lap(f[1]) - adv(f[1])))
    u = wet * (
        east_v
        + TIME_INCREMENT * (cor * north_v - dx(pressure) - adv(f[2]) + VISCOSITY * lap(f[2]))
    )
    v = wet * (
        north_v
        + TIME_INCREMENT * (-cor * east_v - dy(pressure) - adv(f[3]) + VISCOSITY * lap(f[3]))
    )
    return jnp.stack([heat, salt, u, v])


def shards(state, sea_mask, levels):
    n_fields, level_count, tile_rows, tile_cols = state.shape
    depth_index = jnp.arange(level_count, dtype=jnp.int32)[:, None, None]
    depth = jnp.where(sea_mask == 1, levels, 0).astype(jnp.float32)
    channels = jnp.concatenate([state.reshape(n_fields * level_count, tile_rows, tile_cols), depth[None]])
    signs = jnp.array([1.0, 1.0, -1.0, -1.0], dtype=jnp.float32)
    signs = jnp.concatenate([jnp.repeat(signs, level_count), jnp.ones((1,), jnp.float32)])
    wide = gather_wide(channels, signs[:, None, None])

    lat = lax.axis_index("lat")
    total = lax.axis_size("lat") * tile_rows
    first_row = lat * tile_rows

    grown = wide[:, MARGIN:-MARGIN, MARGIN:-MARGIN]
    grown_depth = grown[-1]
    grown_wet = (depth_index < grown_depth[None]).astype(jnp.float32)
    grown_rows = first_row - MARGIN + jnp.arange(tile_rows + 2 * MARGIN, dtype=jnp.int32)
    fields = wide[:-1].reshape(n_fields, level_count, *wide.shape[1:])
    once = advance(fields, grown_wet, coriolis(grown_rows, total))
    south_edge = (lat == 0) & (grown_rows < 0)
    once = jnp.where(south_edge[:, None], 0.0, once)

    wet = (depth_index < depth[None]).astype(jnp.float32)
    own_rows = first_row + jnp.arange(tile_rows, dtype=jnp.int32)
    return advance(once, wet, coriolis(own_rows, total))


def solution(mesh):
    return jax.shard_map(
        shards,
        mesh=mesh,
        in_specs=(P(None, None, "lat", "lon"), P("lat", "lon"), P("lat", "lon")),
        out_specs=P(None, None, "lat", "lon"),
        check_vma=False,
    )
```

```python
import jax
import jax.numpy as jnp
from jax import lax
from jax.sharding import PartitionSpec as P

TIME_INCREMENT = 0.1
SCALAR_MIXING = 0.4
VISCOSITY = 0.4
THERMAL = 0.2
HALINE = 0.8
GRAVITY = 0.1
MARGIN = 2
WIDE = 2 * MARGIN


def coriolis(row_index, total):
    mirrored = jnp.where(row_index >= total, 2 * total - 1 - row_index, row_index)
    return (1.2 * jnp.sin(-1.3 + 2.8 * (mirrored.astype(jnp.float32) + 0.5) / total))[:, None]


def gather_wide(x, signs):
    n_lon = lax.axis_size("lon")
    n_lat = lax.axis_size("lat")

    lat = lax.axis_index("lat")
    odd = lat % 2 == 1
    top_rows = x[:, -WIDE:, :]
    bottom_rows = x[:, :WIDE, :]
    inner = [(i, i + 1) for i in range(1, n_lat - 1, 2)]
    inner = inner + [(j, i) for i, j in inner]
    top = n_lat - 1
    pairs = [(l * n_lat + i, l * n_lat + j) for l in range(n_lon) for i, j in inner]
    pairs = pairs + [(l * n_lat + top, (n_lon - 1 - l) * n_lat + top) for l in range(n_lon)]
    to_even = lax.ppermute(jnp.where(odd, top_rows, bottom_rows), ("lon", "lat"), pairs)
    to_odd = lax.ppermute(
        jnp.where(odd, bottom_rows, top_rows),
        ("lon", "lat"),
        [(l * n_lat + i, l * n_lat + (i ^ 1)) for l in range(n_lon) for i in range(n_lat)],
    )
    folded = jnp.flip(to_even, axis=(1, 2)) * signs
    north = jnp.where(odd, jnp.where(lat == top, folded, to_even), to_odd)
    south = jnp.where(odd, to_odd, to_even)
    lat_wide = jnp.concatenate([south, x, north], axis=1)

    lon = lax.axis_index("lon")
    lon_odd = lon % 2 == 1
    edge_shape = lat_wide[..., :WIDE].shape
    east_cols = lat_wide[..., -WIDE:].reshape(-1)
    west_cols = lat_wide[..., :WIDE].reshape(-1)
    on_chip = lax.ppermute(
        jnp.where(lon_odd, west_cols, east_cols), "lon", [(m, m ^ 1) for m in range(n_lon)]
    )
    across = [(m, (m + 1) % n_lon) for m in range(1, n_lon, 2)]
    across = across + [(j, i) for i, j in across]
    off_chip = lax.ppermute(jnp.where(lon_odd, east_cols, west_cols), "lon", across)
    west = jnp.where(lon_odd, on_chip, off_chip).reshape(edge_shape)
    east = jnp.where(lon_odd, off_chip, on_chip).reshape(edge_shape)
    return lat_wide, west, east


def advance(f, wet, cor):
    rows_n = f.shape[2] - 2 * MARGIN
    cols_n = f.shape[3] - 2 * MARGIN

    def at(g, dr, dc):
        return g[..., MARGIN + dr : MARGIN + dr + rows_n, MARGIN + dc : MARGIN + dc + cols_n]

    def dx(g):
        return (8.0 * (at(g, 0, 1) - at(g, 0, -1)) - (at(g, 0, 2) - at(g, 0, -2))) / 12.0

    def dy(g):
        return (8.0 * (at(g, 1, 0) - at(g, -1, 0)) - (at(g, 2, 0) - at(g, -2, 0))) / 12.0

    def lap(g):
        return at(g, 0, 1) + at(g, 0, -1) + at(g, 1, 0) + at(g, -1, 0) - 4.0 * at(g, 0, 0)

    pressure = GRAVITY * jnp.cumsum(HALINE * f[1] - THERMAL * f[0], axis=0)
    east_v, north_v = at(f[2], 0, 0), at(f[3], 0, 0)

    def adv(g):
        return east_v * dx(g) + north_v * dy(g)

    heat = wet * (at(f[0], 0, 0) + TIME_INCREMENT * (SCALAR_MIXING * lap(f[0]) - adv(f[0])))
    salt = wet * (at(f[1], 0, 0) + TIME_INCREMENT * (SCALAR_MIXING * lap(f[1]) - adv(f[1])))
    u = wet * (
        east_v
        + TIME_INCREMENT * (cor * north_v - dx(pressure) - adv(f[2]) + VISCOSITY * lap(f[2]))
    )
    v = wet * (
        north_v
        + TIME_INCREMENT * (-cor * east_v - dy(pressure) - adv(f[3]) + VISCOSITY * lap(f[3]))
    )
    return jnp.stack([heat, salt, u, v])


def shards(state, sea_mask, levels):
    n_fields, level_count, tile_rows, tile_cols = state.shape
    depth_index = jnp.arange(level_count, dtype=jnp.int32)[:, None, None]
    depth = jnp.where(sea_mask == 1, levels, 0).astype(jnp.float32)
    channels = jnp.concatenate([state.reshape(n_fields * level_count, tile_rows, tile_cols), depth[None]])
    signs = jnp.array([1.0, 1.0, -1.0, -1.0], dtype=jnp.float32)
    signs = jnp.concatenate([jnp.repeat(signs, level_count), jnp.ones((1,), jnp.float32)])
    lat_wide, west, east = gather_wide(channels, signs[:, None, None])

    lat = lax.axis_index("lat")
    total = lax.axis_size("lat") * tile_rows
    first_row = lat * tile_rows
    grown_rows = first_row - MARGIN + jnp.arange(tile_rows + 2 * MARGIN, dtype=jnp.int32)
    grown_cor = coriolis(grown_rows, total)

    def step_once(wide):
        grown_depth = wide[-1, MARGIN:-MARGIN, MARGIN:-MARGIN]
        grown_wet = (depth_index < grown_depth[None]).astype(jnp.float32)
        fields = wide[:-1].reshape(n_fields, level_count, *wide.shape[1:])
        return advance(fields, grown_wet, grown_cor)

    inner = step_once(lat_wide)
    edges = step_once(jnp.concatenate([west, lat_wide[..., :WIDE], lat_wide[..., -WIDE:], east], axis=2))
    span = 2 * MARGIN
    once = jnp.concatenate([edges[..., :span], inner, edges[..., -span:]], axis=3)
    south_edge = (lat == 0) & (grown_rows < 0)
    once = jnp.where(south_edge[:, None], 0.0, once)

    wet = (depth_index < depth[None]).astype(jnp.float32)
    own_rows = first_row + jnp.arange(tile_rows, dtype=jnp.int32)
    return advance(once, wet, coriolis(own_rows, total))


def solution(mesh):
    return jax.shard_map(
        shards,
        mesh=mesh,
        in_specs=(P(None, None, "lat", "lon"), P("lat", "lon"), P("lat", "lon")),
        out_specs=P(None, None, "lat", "lon"),
        check_vma=False,
    )
```

```python
import jax
import jax.numpy as jnp
from jax import lax
from jax.sharding import PartitionSpec as P

TIME_INCREMENT = 0.1
SCALAR_MIXING = 0.4
VISCOSITY = 0.4
THERMAL = 0.2
HALINE = 0.8
GRAVITY = 0.1
MARGIN = 2
WIDE = 2 * MARGIN


def coriolis(row_index, total):
    mirrored = jnp.where(row_index >= total, 2 * total - 1 - row_index, row_index)
    return (1.2 * jnp.sin(-1.3 + 2.8 * (mirrored.astype(jnp.float32) + 0.5) / total))[:, None]


def gather_wide(x, signs):
    n_lon = lax.axis_size("lon")
    n_lat = lax.axis_size("lat")

    lat = lax.axis_index("lat")
    odd = lat % 2 == 1
    top_rows = x[:, -WIDE:, :]
    bottom_rows = x[:, :WIDE, :]
    inner = [(i, i + 1) for i in range(1, n_lat - 1, 2)]
    inner = inner + [(j, i) for i, j in inner]
    top = n_lat - 1
    pairs = [(l * n_lat + i, l * n_lat + j) for l in range(n_lon) for i, j in inner]
    pairs = pairs + [(l * n_lat + top, (n_lon - 1 - l) * n_lat + top) for l in range(n_lon)]
    to_even = lax.ppermute(jnp.where(odd, top_rows, bottom_rows), ("lon", "lat"), pairs)
    to_odd = lax.ppermute(
        jnp.where(odd, bottom_rows, top_rows),
        ("lon", "lat"),
        [(l * n_lat + i, l * n_lat + (i ^ 1)) for l in range(n_lon) for i in range(n_lat)],
    )
    folded = jnp.flip(to_even, axis=(1, 2)) * signs
    north = jnp.where(odd, jnp.where(lat == top, folded, to_even), to_odd)
    south = jnp.where(odd, to_odd, to_even)
    lat_wide = jnp.concatenate([south, x, north], axis=1)

    lon = lax.axis_index("lon")
    lon_odd = lon % 2 == 1
    edge_shape = lat_wide[..., :WIDE].shape
    east_cols = lat_wide[..., -WIDE:].reshape(-1)
    west_cols = lat_wide[..., :WIDE].reshape(-1)
    on_chip = lax.ppermute(
        jnp.where(lon_odd, west_cols, east_cols), "lon", [(m, m ^ 1) for m in range(n_lon)]
    )
    across = [(m, (m + 1) % n_lon) for m in range(1, n_lon, 2)]
    across = across + [(j, i) for i, j in across]
    off_chip = lax.ppermute(jnp.where(lon_odd, east_cols, west_cols), "lon", across)
    west = jnp.where(lon_odd, on_chip, off_chip).reshape(edge_shape)
    east = jnp.where(lon_odd, off_chip, on_chip).reshape(edge_shape)
    return lat_wide, west, east


def advance(f, wet, cor):
    rows_n = f.shape[2] - 2 * MARGIN
    cols_n = f.shape[3] - 2 * MARGIN

    def at(g, dr, dc):
        return g[..., MARGIN + dr : MARGIN + dr + rows_n, MARGIN + dc : MARGIN + dc + cols_n]

    def dx(g):
        return (8.0 * (at(g, 0, 1) - at(g, 0, -1)) - (at(g, 0, 2) - at(g, 0, -2))) / 12.0

    def dy(g):
        return (8.0 * (at(g, 1, 0) - at(g, -1, 0)) - (at(g, 2, 0) - at(g, -2, 0))) / 12.0

    def lap(g):
        return at(g, 0, 1) + at(g, 0, -1) + at(g, 1, 0) + at(g, -1, 0) - 4.0 * at(g, 0, 0)

    pressure = GRAVITY * jnp.cumsum(HALINE * f[1] - THERMAL * f[0], axis=0)
    east_v, north_v = at(f[2], 0, 0), at(f[3], 0, 0)

    def adv(g):
        return east_v * dx(g) + north_v * dy(g)

    heat = wet * (at(f[0], 0, 0) + TIME_INCREMENT * (SCALAR_MIXING * lap(f[0]) - adv(f[0])))
    salt = wet * (at(f[1], 0, 0) + TIME_INCREMENT * (SCALAR_MIXING * lap(f[1]) - adv(f[1])))
    u = wet * (
        east_v
        + TIME_INCREMENT * (cor * north_v - dx(pressure) - adv(f[2]) + VISCOSITY * lap(f[2]))
    )
    v = wet * (
        north_v
        + TIME_INCREMENT * (-cor * east_v - dy(pressure) - adv(f[3]) + VISCOSITY * lap(f[3]))
    )
    return jnp.stack([heat, salt, u, v])


def shards(state, sea_mask, levels):
    n_fields, level_count, tile_rows, tile_cols = state.shape
    depth_index = jnp.arange(level_count, dtype=jnp.int32)[:, None, None]
    depth = jnp.where(sea_mask == 1, levels, 0).astype(jnp.float32)
    channels = jnp.concatenate([state.reshape(n_fields * level_count, tile_rows, tile_cols), depth[None]])
    signs = jnp.array([1.0, 1.0, -1.0, -1.0], dtype=jnp.float32)
    signs = jnp.concatenate([jnp.repeat(signs, level_count), jnp.ones((1,), jnp.float32)])
    lat_wide, west, east = gather_wide(channels, signs[:, None, None])

    lat = lax.axis_index("lat")
    total = lax.axis_size("lat") * tile_rows
    first_row = lat * tile_rows
    grown_rows = first_row - MARGIN + jnp.arange(tile_rows + 2 * MARGIN, dtype=jnp.int32)
    grown_cor = coriolis(grown_rows, total)

    def step_once(wide, tie=0.0):
        grown_depth = wide[-1, MARGIN:-MARGIN, MARGIN:-MARGIN] + tie
        grown_wet = (depth_index < grown_depth[None]).astype(jnp.float32)
        fields = wide[:-1].reshape(n_fields, level_count, *wide.shape[1:])
        return advance(fields, grown_wet, grown_cor)

    inner = step_once(lat_wide, 0.0 * (west[-1, :1, :1] + east[-1, :1, :1]))
    edges = step_once(jnp.concatenate([west, lat_wide[..., :WIDE], lat_wide[..., -WIDE:], east], axis=2))
    span = 2 * MARGIN
    once = jnp.concatenate([edges[..., :span], inner, edges[..., -span:]], axis=3)
    south_edge = (lat == 0) & (grown_rows < 0)
    once = jnp.where(south_edge[:, None], 0.0, once)

    wet = (depth_index < depth[None]).astype(jnp.float32)
    own_rows = first_row + jnp.arange(tile_rows, dtype=jnp.int32)
    return advance(once, wet, coriolis(own_rows, total))


def solution(mesh):
    return jax.shard_map(
        shards,
        mesh=mesh,
        in_specs=(P(None, None, "lat", "lon"), P("lat", "lon"), P("lat", "lon")),
        out_specs=P(None, None, "lat", "lon"),
        check_vma=False,
    )
```

```python
import jax
import jax.numpy as jnp
from jax import lax
from jax.experimental import pallas as pl
from jax.experimental.pallas import tpu as pltpu
from jax.sharding import PartitionSpec as P

TIME_INCREMENT = 0.1
SCALAR_MIXING = 0.4
VISCOSITY = 0.4
THERMAL = 0.2
HALINE = 0.8
GRAVITY = 0.1
MARGIN = 2
INTERPRET = False
WIDE = 2 * MARGIN


def coriolis(row_index, total):
    mirrored = jnp.where(row_index >= total, 2 * total - 1 - row_index, row_index)
    return (1.2 * jnp.sin(-1.3 + 2.8 * (mirrored.astype(jnp.float32) + 0.5) / total))[:, None]


def gather_wide(x, signs):
    n_lon = lax.axis_size("lon")
    n_lat = lax.axis_size("lat")

    lat = lax.axis_index("lat")
    odd = lat % 2 == 1
    top_rows = x[:, -WIDE:, :]
    bottom_rows = x[:, :WIDE, :]
    inner = [(i, i + 1) for i in range(1, n_lat - 1, 2)]
    inner = inner + [(j, i) for i, j in inner]
    top = n_lat - 1
    pairs = [(l * n_lat + i, l * n_lat + j) for l in range(n_lon) for i, j in inner]
    pairs = pairs + [(l * n_lat + top, (n_lon - 1 - l) * n_lat + top) for l in range(n_lon)]
    to_even = lax.ppermute(jnp.where(odd, top_rows, bottom_rows), ("lon", "lat"), pairs)
    to_odd = lax.ppermute(
        jnp.where(odd, bottom_rows, top_rows),
        ("lon", "lat"),
        [(l * n_lat + i, l * n_lat + (i ^ 1)) for l in range(n_lon) for i in range(n_lat)],
    )
    folded = jnp.flip(to_even, axis=(1, 2)) * signs
    north = jnp.where(odd, jnp.where(lat == top, folded, to_even), to_odd)
    south = jnp.where(odd, to_odd, to_even)
    lat_wide = jnp.concatenate([south, x, north], axis=1)

    lon = lax.axis_index("lon")
    lon_odd = lon % 2 == 1
    edge_shape = lat_wide[..., :WIDE].shape
    east_cols = lat_wide[..., -WIDE:].reshape(-1)
    west_cols = lat_wide[..., :WIDE].reshape(-1)
    on_chip = lax.ppermute(
        jnp.where(lon_odd, west_cols, east_cols), "lon", [(m, m ^ 1) for m in range(n_lon)]
    )
    across = [(m, (m + 1) % n_lon) for m in range(1, n_lon, 2)]
    across = across + [(j, i) for i, j in across]
    off_chip = lax.ppermute(jnp.where(lon_odd, east_cols, west_cols), "lon", across)
    west = jnp.where(lon_odd, on_chip, off_chip).reshape(edge_shape)
    east = jnp.where(lon_odd, off_chip, on_chip).reshape(edge_shape)
    return jnp.concatenate([west, lat_wide, east], axis=2)


def advance(f, wet, cor):
    rows_n = f.shape[2] - 2 * MARGIN
    cols_n = f.shape[3] - 2 * MARGIN

    def at(g, dr, dc):
        return g[..., MARGIN + dr : MARGIN + dr + rows_n, MARGIN + dc : MARGIN + dc + cols_n]

    def dx(g):
        return (8.0 * (at(g, 0, 1) - at(g, 0, -1)) - (at(g, 0, 2) - at(g, 0, -2))) / 12.0

    def dy(g):
        return (8.0 * (at(g, 1, 0) - at(g, -1, 0)) - (at(g, 2, 0) - at(g, -2, 0))) / 12.0

    def lap(g):
        return at(g, 0, 1) + at(g, 0, -1) + at(g, 1, 0) + at(g, -1, 0) - 4.0 * at(g, 0, 0)

    pressure = GRAVITY * jnp.cumsum(HALINE * f[1] - THERMAL * f[0], axis=0)
    east_v, north_v = at(f[2], 0, 0), at(f[3], 0, 0)

    def adv(g):
        return east_v * dx(g) + north_v * dy(g)

    heat = wet * (at(f[0], 0, 0) + TIME_INCREMENT * (SCALAR_MIXING * lap(f[0]) - adv(f[0])))
    salt = wet * (at(f[1], 0, 0) + TIME_INCREMENT * (SCALAR_MIXING * lap(f[1]) - adv(f[1])))
    u = wet * (
        east_v
        + TIME_INCREMENT * (cor * north_v - dx(pressure) - adv(f[2]) + VISCOSITY * lap(f[2]))
    )
    v = wet * (
        north_v
        + TIME_INCREMENT * (-cor * east_v - dy(pressure) - adv(f[3]) + VISCOSITY * lap(f[3]))
    )
    return jnp.stack([heat, salt, u, v])


def two_steps_kernel(wide_ref, cor1_ref, keep1_ref, cor2_ref, out_ref, once_ref, sum1_ref, p1_ref, sum2_ref, p2_ref):
    n_fields, level_count, rows2, cols2 = out_ref.shape
    rows1, cols1 = rows2 + 2 * MARGIN, cols2 + 2 * MARGIN
    depth_ch = n_fields * level_count
    sum1_ref[...] = jnp.zeros(sum1_ref.shape, jnp.float32)
    sum2_ref[...] = jnp.zeros(sum2_ref.shape, jnp.float32)

    def stencils(src, dst_p, wet, cor, rows, cols, chans):
        def at(c, dr, dc):
            return src(c, MARGIN + dr, rows, MARGIN + dc, cols)

        def at_p(dr, dc):
            return dst_p[pl.ds(MARGIN + dr, rows), pl.ds(MARGIN + dc, cols)]

        def dx(g):
            return (8.0 * (g(0, 1) - g(0, -1)) - (g(0, 2) - g(0, -2))) / 12.0

        def dy(g):
            return (8.0 * (g(1, 0) - g(-1, 0)) - (g(2, 0) - g(-2, 0))) / 12.0

        def field(c):
            return lambda dr, dc: at(c, dr, dc)

        def lap(g):
            return g(0, 1) + g(0, -1) + g(1, 0) + g(-1, 0) - 4.0 * g(0, 0)

        heat_c, salt_c, u_c, v_c = chans
        east_v, north_v = at(u_c, 0, 0), at(v_c, 0, 0)

        def adv(g):
            return east_v * dx(g) + north_v * dy(g)

        t, sa, u, v = field(heat_c), field(salt_c), field(u_c), field(v_c)
        heat = wet * (t(0, 0) + TIME_INCREMENT * (SCALAR_MIXING * lap(t) - adv(t)))
        salt = wet * (sa(0, 0) + TIME_INCREMENT * (SCALAR_MIXING * lap(sa) - adv(sa)))
        new_u = wet * (
            east_v + TIME_INCREMENT * (cor * north_v - dx(at_p) - adv(u) + VISCOSITY * lap(u))
        )
        new_v = wet * (
            north_v + TIME_INCREMENT * (-cor * east_v - dy(at_p) - adv(v) + VISCOSITY * lap(v))
        )
        return heat, salt, new_u, new_v

    def level(k, carry):
        kf = k.astype(jnp.float32)

        def wide_at(c, r0, nr, c0, nc):
            return wide_ref[c, pl.ds(r0, nr), pl.ds(c0, nc)]

        chans = (k, level_count + k, 2 * level_count + k, 3 * level_count + k)
        sum1_ref[...] += HALINE * wide_ref[chans[1]] - THERMAL * wide_ref[chans[0]]
        p1_ref[...] = GRAVITY * sum1_ref[...]
        depth1 = wide_ref[depth_ch, pl.ds(MARGIN, rows1), pl.ds(MARGIN, cols1)]
        wet1 = jnp.where(kf < depth1, 1.0, 0.0)
        keep = keep1_ref[...]
        once = stencils(wide_at, p1_ref, wet1, cor1_ref[...], rows1, cols1, chans)
        for f in range(n_fields):
            once_ref[f] = jnp.where(keep > 0.5, once[f], 0.0)

        def once_at(c, r0, nr, c0, nc):
            return once_ref[c, pl.ds(r0, nr), pl.ds(c0, nc)]

        sum2_ref[...] += HALINE * once_ref[1] - THERMAL * once_ref[0]
        p2_ref[...] = GRAVITY * sum2_ref[...]
        depth2 = wide_ref[depth_ch, pl.ds(2 * MARGIN, rows2), pl.ds(2 * MARGIN, cols2)]
        wet2 = jnp.where(kf < depth2, 1.0, 0.0)
        twice = stencils(once_at, p2_ref, wet2, cor2_ref[...], rows2, cols2, (0, 1, 2, 3))
        for f in range(n_fields):
            out_ref[f, k] = twice[f]
        return carry

    lax.fori_loop(0, level_count, level, 0)


def shards(state, sea_mask, levels):
    n_fields, level_count, tile_rows, tile_cols = state.shape
    depth_index = jnp.arange(level_count, dtype=jnp.int32)[:, None, None]
    depth = jnp.where(sea_mask == 1, levels, 0).astype(jnp.float32)
    channels = jnp.concatenate([state.reshape(n_fields * level_count, tile_rows, tile_cols), depth[None]])
    signs = jnp.array([1.0, 1.0, -1.0, -1.0], dtype=jnp.float32)
    signs = jnp.concatenate([jnp.repeat(signs, level_count), jnp.ones((1,), jnp.float32)])
    wide = gather_wide(channels, signs[:, None, None])

    lat = lax.axis_index("lat")
    total = lax.axis_size("lat") * tile_rows
    first_row = lat * tile_rows
    grown_rows = first_row - MARGIN + jnp.arange(tile_rows + 2 * MARGIN, dtype=jnp.int32)
    grown_cols = tile_cols + 2 * MARGIN
    cor1 = jnp.broadcast_to(coriolis(grown_rows, total), (tile_rows + 2 * MARGIN, grown_cols))
    keep1 = jnp.broadcast_to(
        jnp.where((lat == 0) & (grown_rows < 0), 0.0, 1.0)[:, None], cor1.shape
    )
    own_rows = first_row + jnp.arange(tile_rows, dtype=jnp.int32)
    cor2 = jnp.broadcast_to(coriolis(own_rows, total), (tile_rows, tile_cols))
    grown = (n_fields, tile_rows + 2 * MARGIN, grown_cols)
    wide_shape = (tile_rows + 2 * WIDE, tile_cols + 2 * WIDE)
    return pl.pallas_call(
        two_steps_kernel,
        out_shape=jax.ShapeDtypeStruct(state.shape, jnp.float32),
        scratch_shapes=[
            pltpu.VMEM(grown, jnp.float32),
            pltpu.VMEM(wide_shape, jnp.float32),
            pltpu.VMEM(wide_shape, jnp.float32),
            pltpu.VMEM(grown[1:], jnp.float32),
            pltpu.VMEM(grown[1:], jnp.float32),
        ],
        interpret=INTERPRET,
    )(wide, cor1, keep1, cor2)

def solution(mesh):
    return jax.shard_map(
        shards,
        mesh=mesh,
        in_specs=(P(None, None, "lat", "lon"), P("lat", "lon"), P("lat", "lon")),
        out_specs=P(None, None, "lat", "lon"),
        check_vma=False,
    )
```

```python
import jax
import jax.numpy as jnp
from jax import lax
from jax.sharding import PartitionSpec as P

TIME_INCREMENT = 0.1
SCALAR_MIXING = 0.4
VISCOSITY = 0.4
THERMAL = 0.2
HALINE = 0.8
GRAVITY = 0.1
MARGIN = 2
WIDE = 2 * MARGIN


def coriolis(row_index, total):
    mirrored = jnp.where(row_index >= total, 2 * total - 1 - row_index, row_index)
    return (1.2 * jnp.sin(-1.3 + 2.8 * (mirrored.astype(jnp.float32) + 0.5) / total))[:, None]


def gather_wide(x, signs):
    n_lon = lax.axis_size("lon")
    n_lat = lax.axis_size("lat")

    lat = lax.axis_index("lat")
    odd = lat % 2 == 1
    inner = [(i, i + 1) for i in range(1, n_lat - 1, 2)]
    inner = inner + [(j, i) for i, j in inner]
    top = n_lat - 1
    pairs = [(l * n_lat + i, l * n_lat + j) for l in range(n_lon) for i, j in inner]
    pairs = pairs + [(l * n_lat + top, (n_lon - 1 - l) * n_lat + top) for l in range(n_lon)]
    to_even = lax.ppermute(x, ("lon", "lat"), pairs)
    to_odd = lax.ppermute(
        x,
        ("lon", "lat"),
        [(l * n_lat + i, l * n_lat + (i ^ 1)) for l in range(n_lon) for i in range(n_lat)],
    )
    folded = jnp.flip(to_even[:, -WIDE:, :], axis=(1, 2)) * signs
    north = jnp.where(
        odd, jnp.where(lat == top, folded, to_even[:, :WIDE, :]), to_odd[:, :WIDE, :]
    )
    south = jnp.where(odd, to_odd[:, -WIDE:, :], to_even[:, -WIDE:, :])
    lat_wide = jnp.concatenate([south, x, north], axis=1)

    lon = lax.axis_index("lon")
    lon_odd = lon % 2 == 1
    edge_shape = lat_wide[..., :WIDE].shape
    east_cols = lat_wide[..., -WIDE:].reshape(-1)
    west_cols = lat_wide[..., :WIDE].reshape(-1)
    on_chip = lax.ppermute(
        jnp.where(lon_odd, west_cols, east_cols), "lon", [(m, m ^ 1) for m in range(n_lon)]
    )
    across = [(m, (m + 1) % n_lon) for m in range(1, n_lon, 2)]
    across = across + [(j, i) for i, j in across]
    off_chip = lax.ppermute(jnp.where(lon_odd, east_cols, west_cols), "lon", across)
    west = jnp.where(lon_odd, on_chip, off_chip).reshape(edge_shape)
    east = jnp.where(lon_odd, off_chip, on_chip).reshape(edge_shape)
    return jnp.concatenate([west, lat_wide, east], axis=2)


def advance(f, wet, cor):
    rows_n = f.shape[2] - 2 * MARGIN
    cols_n = f.shape[3] - 2 * MARGIN

    def at(g, dr, dc):
        return g[..., MARGIN + dr : MARGIN + dr + rows_n, MARGIN + dc : MARGIN + dc + cols_n]

    def dx(g):
        return (8.0 * (at(g, 0, 1) - at(g, 0, -1)) - (at(g, 0, 2) - at(g, 0, -2))) / 12.0

    def dy(g):
        return (8.0 * (at(g, 1, 0) - at(g, -1, 0)) - (at(g, 2, 0) - at(g, -2, 0))) / 12.0

    def lap(g):
        return at(g, 0, 1) + at(g, 0, -1) + at(g, 1, 0) + at(g, -1, 0) - 4.0 * at(g, 0, 0)

    pressure = GRAVITY * jnp.cumsum(HALINE * f[1] - THERMAL * f[0], axis=0)
    east_v, north_v = at(f[2], 0, 0), at(f[3], 0, 0)

    def adv(g):
        return east_v * dx(g) + north_v * dy(g)

    heat = wet * (at(f[0], 0, 0) + TIME_INCREMENT * (SCALAR_MIXING * lap(f[0]) - adv(f[0])))
    salt = wet * (at(f[1], 0, 0) + TIME_INCREMENT * (SCALAR_MIXING * lap(f[1]) - adv(f[1])))
    u = wet * (
        east_v
        + TIME_INCREMENT * (cor * north_v - dx(pressure) - adv(f[2]) + VISCOSITY * lap(f[2]))
    )
    v = wet * (
        north_v
        + TIME_INCREMENT * (-cor * east_v - dy(pressure) - adv(f[3]) + VISCOSITY * lap(f[3]))
    )
    return jnp.stack([heat, salt, u, v])


def shards(state, sea_mask, levels):
    n_fields, level_count, tile_rows, tile_cols = state.shape
    depth_index = jnp.arange(level_count, dtype=jnp.int32)[:, None, None]
    depth = jnp.where(sea_mask == 1, levels, 0).astype(jnp.float32)
    channels = jnp.concatenate([state.reshape(n_fields * level_count, tile_rows, tile_cols), depth[None]])
    signs = jnp.array([1.0, 1.0, -1.0, -1.0], dtype=jnp.float32)
    signs = jnp.concatenate([jnp.repeat(signs, level_count), jnp.ones((1,), jnp.float32)])
    wide = gather_wide(channels, signs[:, None, None])

    lat = lax.axis_index("lat")
    total = lax.axis_size("lat") * tile_rows
    first_row = lat * tile_rows

    grown = wide[:, MARGIN:-MARGIN, MARGIN:-MARGIN]
    grown_depth = grown[-1]
    grown_wet = (depth_index < grown_depth[None]).astype(jnp.float32)
    grown_rows = first_row - MARGIN + jnp.arange(tile_rows + 2 * MARGIN, dtype=jnp.int32)
    fields = wide[:-1].reshape(n_fields, level_count, *wide.shape[1:])
    once = advance(fields, grown_wet, coriolis(grown_rows, total))
    south_edge = (lat == 0) & (grown_rows < 0)
    once = jnp.where(south_edge[:, None], 0.0, once)

    wet = (depth_index < depth[None]).astype(jnp.float32)
    own_rows = first_row + jnp.arange(tile_rows, dtype=jnp.int32)
    return advance(once, wet, coriolis(own_rows, total))


def solution(mesh):
    return jax.shard_map(
        shards,
        mesh=mesh,
        in_specs=(P(None, None, "lat", "lon"), P("lat", "lon"), P("lat", "lon")),
        out_specs=P(None, None, "lat", "lon"),
        check_vma=False,
    )
```

```python
import jax
import jax.numpy as jnp
from jax import lax
from jax.sharding import PartitionSpec as P

TIME_INCREMENT = 0.1
SCALAR_MIXING = 0.4
VISCOSITY = 0.4
THERMAL = 0.2
HALINE = 0.8
GRAVITY = 0.1
MARGIN = 2
WIDE = 2 * MARGIN


def coriolis(row_index, total):
    mirrored = jnp.where(row_index >= total, 2 * total - 1 - row_index, row_index)
    return (1.2 * jnp.sin(-1.3 + 2.8 * (mirrored.astype(jnp.float32) + 0.5) / total))[:, None]


def lat_exchange(x, signs, far):
    n_lon = lax.axis_size("lon")
    n_lat = lax.axis_size("lat")
    lat = lax.axis_index("lat")
    odd = lat % 2 == 1
    rows = x.shape[1]
    skip = MARGIN if far else 0
    top_rows = x[:, rows - MARGIN - skip : rows - skip, :]
    bottom_rows = x[:, skip : skip + MARGIN, :]
    inner = [(i, i + 1) for i in range(1, n_lat - 1, 2)]
    inner = inner + [(j, i) for i, j in inner]
    top = n_lat - 1
    pairs = [(l * n_lat + i, l * n_lat + j) for l in range(n_lon) for i, j in inner]
    pairs = pairs + [(l * n_lat + top, (n_lon - 1 - l) * n_lat + top) for l in range(n_lon)]
    to_even = lax.ppermute(jnp.where(odd, top_rows, bottom_rows), ("lon", "lat"), pairs)
    to_odd = lax.ppermute(
        jnp.where(odd, bottom_rows, top_rows),
        ("lon", "lat"),
        [(l * n_lat + i, l * n_lat + (i ^ 1)) for l in range(n_lon) for i in range(n_lat)],
    )
    folded = jnp.flip(to_even, axis=(1, 2)) * signs
    north = jnp.where(odd, jnp.where(lat == top, folded, to_even), to_odd)
    south = jnp.where(odd, to_odd, to_even)
    return south, north


def lon_exchange(x):
    n_lon = lax.axis_size("lon")
    lon = lax.axis_index("lon")
    lon_odd = lon % 2 == 1
    edge_shape = x[..., :WIDE].shape
    east_cols = x[..., -WIDE:].reshape(-1)
    west_cols = x[..., :WIDE].reshape(-1)
    on_chip = lax.ppermute(
        jnp.where(lon_odd, west_cols, east_cols), "lon", [(m, m ^ 1) for m in range(n_lon)]
    )
    across = [(m, (m + 1) % n_lon) for m in range(1, n_lon, 2)]
    across = across + [(j, i) for i, j in across]
    off_chip = lax.ppermute(jnp.where(lon_odd, east_cols, west_cols), "lon", across)
    west = jnp.where(lon_odd, on_chip, off_chip).reshape(edge_shape)
    east = jnp.where(lon_odd, off_chip, on_chip).reshape(edge_shape)
    return west, east


def gather_wide(x, signs):
    south, north = lat_exchange(x, signs, False)
    lat_wide = jnp.concatenate([south, x, north], axis=1)
    west, east = lon_exchange(lat_wide)
    tie = 0.0 * (south[:-1, :1, :1] + north[:-1, :1, :1])
    far_south, far_north = lat_exchange(x[:-1] + tie, signs[:-1], True)
    middle = jnp.concatenate([west, lat_wide, east], axis=2)
    fill = ((0, 1), (0, 0), (WIDE, WIDE))
    return jnp.concatenate([jnp.pad(far_south, fill), middle, jnp.pad(far_north, fill)], axis=1)


def advance(f, wet, cor):
    rows_n = f.shape[2] - 2 * MARGIN
    cols_n = f.shape[3] - 2 * MARGIN

    def at(g, dr, dc):
        return g[..., MARGIN + dr : MARGIN + dr + rows_n, MARGIN + dc : MARGIN + dc + cols_n]

    def dx(g):
        return (8.0 * (at(g, 0, 1) - at(g, 0, -1)) - (at(g, 0, 2) - at(g, 0, -2))) / 12.0

    def dy(g):
        return (8.0 * (at(g, 1, 0) - at(g, -1, 0)) - (at(g, 2, 0) - at(g, -2, 0))) / 12.0

    def lap(g):
        return at(g, 0, 1) + at(g, 0, -1) + at(g, 1, 0) + at(g, -1, 0) - 4.0 * at(g, 0, 0)

    pressure = GRAVITY * jnp.cumsum(HALINE * f[1] - THERMAL * f[0], axis=0)
    east_v, north_v = at(f[2], 0, 0), at(f[3], 0, 0)

    def adv(g):
        return east_v * dx(g) + north_v * dy(g)

    heat = wet * (at(f[0], 0, 0) + TIME_INCREMENT * (SCALAR_MIXING * lap(f[0]) - adv(f[0])))
    salt = wet * (at(f[1], 0, 0) + TIME_INCREMENT * (SCALAR_MIXING * lap(f[1]) - adv(f[1])))
    u = wet * (
        east_v
        + TIME_INCREMENT * (cor * north_v - dx(pressure) - adv(f[2]) + VISCOSITY * lap(f[2]))
    )
    v = wet * (
        north_v
        + TIME_INCREMENT * (-cor * east_v - dy(pressure) - adv(f[3]) + VISCOSITY * lap(f[3]))
    )
    return jnp.stack([heat, salt, u, v])


def shards(state, sea_mask, levels):
    n_fields, level_count, tile_rows, tile_cols = state.shape
    depth_index = jnp.arange(level_count, dtype=jnp.int32)[:, None, None]
    depth = jnp.where(sea_mask == 1, levels, 0).astype(jnp.float32)
    channels = jnp.concatenate([state.reshape(n_fields * level_count, tile_rows, tile_cols), depth[None]])
    signs = jnp.array([1.0, 1.0, -1.0, -1.0], dtype=jnp.float32)
    signs = jnp.concatenate([jnp.repeat(signs, level_count), jnp.ones((1,), jnp.float32)])
    wide = gather_wide(channels, signs[:, None, None])

    lat = lax.axis_index("lat")
    total = lax.axis_size("lat") * tile_rows
    first_row = lat * tile_rows

    grown = wide[:, MARGIN:-MARGIN, MARGIN:-MARGIN]
    grown_depth = grown[-1]
    grown_wet = (depth_index < grown_depth[None]).astype(jnp.float32)
    grown_rows = first_row - MARGIN + jnp.arange(tile_rows + 2 * MARGIN, dtype=jnp.int32)
    fields = wide[:-1].reshape(n_fields, level_count, *wide.shape[1:])
    once = advance(fields, grown_wet, coriolis(grown_rows, total))
    south_edge = (lat == 0) & (grown_rows < 0)
    once = jnp.where(south_edge[:, None], 0.0, once)

    wet = (depth_index < depth[None]).astype(jnp.float32)
    own_rows = first_row + jnp.arange(tile_rows, dtype=jnp.int32)
    return advance(once, wet, coriolis(own_rows, total))


def solution(mesh):
    return jax.shard_map(
        shards,
        mesh=mesh,
        in_specs=(P(None, None, "lat", "lon"), P("lat", "lon"), P("lat", "lon")),
        out_specs=P(None, None, "lat", "lon"),
        check_vma=False,
    )
```

```python
import jax
import jax.numpy as jnp
from jax import lax
from jax.sharding import PartitionSpec as P

TIME_INCREMENT = 0.1
SCALAR_MIXING = 0.4
VISCOSITY = 0.4
THERMAL = 0.2
HALINE = 0.8
GRAVITY = 0.1
MARGIN = 2
WIDE = 2 * MARGIN


def coriolis(row_index, total):
    mirrored = jnp.where(row_index >= total, 2 * total - 1 - row_index, row_index)
    return (1.2 * jnp.sin(-1.3 + 2.8 * (mirrored.astype(jnp.float32) + 0.5) / total))[:, None]


def gather_wide(x, signs):
    n_lon = lax.axis_size("lon")
    n_lat = lax.axis_size("lat")

    lat = lax.axis_index("lat")
    odd = lat % 2 == 1
    top_rows = x[:, -WIDE:, :]
    bottom_rows = x[:, :WIDE, :]
    inner = [(i, i + 1) for i in range(1, n_lat - 1, 2)]
    inner = inner + [(j, i) for i, j in inner]
    top = n_lat - 1
    pairs = [(l * n_lat + i, l * n_lat + j) for l in range(n_lon) for i, j in inner]
    pairs = pairs + [(l * n_lat + top, (n_lon - 1 - l) * n_lat + top) for l in range(n_lon)]
    to_even = lax.ppermute(jnp.where(odd, top_rows, bottom_rows), ("lon", "lat"), pairs)
    to_odd = lax.ppermute(
        jnp.where(odd, bottom_rows, top_rows),
        ("lon", "lat"),
        [(l * n_lat + i, l * n_lat + (i ^ 1)) for l in range(n_lon) for i in range(n_lat)],
    )
    folded = jnp.flip(to_even, axis=(1, 2)) * signs
    north = jnp.where(odd, jnp.where(lat == top, folded, to_even), to_odd)
    south = jnp.where(odd, to_odd, to_even)
    lat_wide = jnp.concatenate([south, x, north], axis=1)

    lon = lax.axis_index("lon")
    lon_odd = lon % 2 == 1
    edge_shape = lat_wide[..., :WIDE].shape
    east_cols = lat_wide[..., -WIDE:].reshape(-1)
    west_cols = lat_wide[..., :WIDE].reshape(-1)
    on_chip = lax.ppermute(
        jnp.where(lon_odd, west_cols, east_cols), "lon", [(m, m ^ 1) for m in range(n_lon)]
    )
    across = [(m, (m + 1) % n_lon) for m in range(1, n_lon, 2)]
    across = across + [(j, i) for i, j in across]
    off_chip = lax.ppermute(jnp.where(lon_odd, east_cols, west_cols), "lon", across)
    west = jnp.where(lon_odd, on_chip, off_chip).reshape(edge_shape)
    east = jnp.where(lon_odd, off_chip, on_chip).reshape(edge_shape)
    wide_state = jnp.concatenate([west[:-1], lat_wide[:-1], east[:-1]], axis=2)
    wide_depth = jnp.concatenate([west[-1], lat_wide[-1], east[-1]], axis=1)
    return wide_state, wide_depth


def advance(f, wet, cor):
    rows_n = f.shape[2] - 2 * MARGIN
    cols_n = f.shape[3] - 2 * MARGIN

    def at(g, dr, dc):
        return g[..., MARGIN + dr : MARGIN + dr + rows_n, MARGIN + dc : MARGIN + dc + cols_n]

    def dx(g):
        return (8.0 * (at(g, 0, 1) - at(g, 0, -1)) - (at(g, 0, 2) - at(g, 0, -2))) / 12.0

    def dy(g):
        return (8.0 * (at(g, 1, 0) - at(g, -1, 0)) - (at(g, 2, 0) - at(g, -2, 0))) / 12.0

    def lap(g):
        return at(g, 0, 1) + at(g, 0, -1) + at(g, 1, 0) + at(g, -1, 0) - 4.0 * at(g, 0, 0)

    pressure = GRAVITY * jnp.cumsum(HALINE * f[1] - THERMAL * f[0], axis=0)
    centre = at(f, 0, 0)
    east_v, north_v = centre[2], centre[3]
    advection = east_v * dx(f) + north_v * dy(f)
    mixing = jnp.array([SCALAR_MIXING, SCALAR_MIXING, VISCOSITY, VISCOSITY], jnp.float32)
    tendency = mixing.reshape(4, 1, 1, 1) * lap(f) - advection
    still = jnp.zeros_like(east_v)
    forcing = jnp.stack(
        [still, still, cor * north_v - dx(pressure), -cor * east_v - dy(pressure)]
    )
    return wet * (centre + TIME_INCREMENT * (tendency + forcing))

def shards(state, sea_mask, levels):
    n_fields, level_count, tile_rows, tile_cols = state.shape
    depth_index = jnp.arange(level_count, dtype=jnp.int32)[:, None, None]
    depth = jnp.where(sea_mask == 1, levels, 0).astype(jnp.float32)
    channels = jnp.concatenate([state.reshape(n_fields * level_count, tile_rows, tile_cols), depth[None]])
    signs = jnp.array([1.0, 1.0, -1.0, -1.0], dtype=jnp.float32)
    signs = jnp.concatenate([jnp.repeat(signs, level_count), jnp.ones((1,), jnp.float32)])
    wide_state, wide_depth = gather_wide(channels, signs[:, None, None])

    lat = lax.axis_index("lat")
    total = lax.axis_size("lat") * tile_rows
    first_row = lat * tile_rows

    grown_depth = wide_depth[MARGIN:-MARGIN, MARGIN:-MARGIN]
    grown_wet = (depth_index < grown_depth[None]).astype(jnp.float32)
    grown_rows = first_row - MARGIN + jnp.arange(tile_rows + 2 * MARGIN, dtype=jnp.int32)
    fields = wide_state.reshape(n_fields, level_count, *wide_state.shape[1:])
    once = advance(fields, grown_wet, coriolis(grown_rows, total))
    south_edge = (lat == 0) & (grown_rows < 0)
    once = jnp.where(south_edge[:, None], 0.0, once)

    wet = (depth_index < depth[None]).astype(jnp.float32)
    own_rows = first_row + jnp.arange(tile_rows, dtype=jnp.int32)
    return advance(once, wet, coriolis(own_rows, total))


def solution(mesh):
    return jax.shard_map(
        shards,
        mesh=mesh,
        in_specs=(P(None, None, "lat", "lon"), P("lat", "lon"), P("lat", "lon")),
        out_specs=P(None, None, "lat", "lon"),
        check_vma=False,
    )
```

```python
import jax
import jax.numpy as jnp
from jax import lax
from jax.sharding import PartitionSpec as P

TIME_INCREMENT = 0.1
SCALAR_MIXING = 0.4
VISCOSITY = 0.4
THERMAL = 0.2
HALINE = 0.8
GRAVITY = 0.1
MARGIN = 2
WIDE = 2 * MARGIN


def coriolis(row_index, total):
    mirrored = jnp.where(row_index >= total, 2 * total - 1 - row_index, row_index)
    return (1.2 * jnp.sin(-1.3 + 2.8 * (mirrored.astype(jnp.float32) + 0.5) / total))[:, None]


def gather_wide(x, signs):
    n_lon = lax.axis_size("lon")
    n_lat = lax.axis_size("lat")

    lat = lax.axis_index("lat")
    odd = lat % 2 == 1
    top_rows = x[:, -WIDE:, :]
    bottom_rows = x[:, :WIDE, :]
    inner = [(i, i + 1) for i in range(1, n_lat - 1, 2)]
    inner = inner + [(j, i) for i, j in inner]
    top = n_lat - 1
    pairs = [(l * n_lat + i, l * n_lat + j) for l in range(n_lon) for i, j in inner]
    pairs = pairs + [(l * n_lat + top, (n_lon - 1 - l) * n_lat + top) for l in range(n_lon)]
    to_even = lax.ppermute(jnp.where(odd, top_rows, bottom_rows), ("lon", "lat"), pairs)
    to_odd = lax.ppermute(
        jnp.where(odd, bottom_rows, top_rows),
        ("lon", "lat"),
        [(l * n_lat + i, l * n_lat + (i ^ 1)) for l in range(n_lon) for i in range(n_lat)],
    )
    folded = jnp.flip(to_even, axis=(1, 2)) * signs
    north = jnp.where(odd, jnp.where(lat == top, folded, to_even), to_odd)
    south = jnp.where(odd, to_odd, to_even)
    lat_wide = jnp.concatenate([south, x, north], axis=1)

    lon = lax.axis_index("lon")
    lon_odd = lon % 2 == 1
    edge_shape = lat_wide[..., :WIDE].shape
    east_cols = lat_wide[..., -WIDE:].reshape(-1)
    west_cols = lat_wide[..., :WIDE].reshape(-1)
    across = [(m, (m + 1) % n_lon) for m in range(1, n_lon, 2)]
    across = across + [(j, i) for i, j in across]
    off_send = jnp.where(lon_odd, east_cols, west_cols)
    off_chip = lax.ppermute(off_send, "lon", across)
    on_send = jnp.where(lon_odd, west_cols, east_cols) + 0.0 * off_send[:1]
    on_chip = lax.ppermute(on_send, "lon", [(m, m ^ 1) for m in range(n_lon)])
    west = jnp.where(lon_odd, on_chip, off_chip).reshape(edge_shape)
    east = jnp.where(lon_odd, off_chip, on_chip).reshape(edge_shape)
    wide_state = jnp.concatenate([west[:-1], lat_wide[:-1], east[:-1]], axis=2)
    wide_depth = jnp.concatenate([west[-1], lat_wide[-1], east[-1]], axis=1)
    return wide_state, wide_depth


def advance(f, wet, cor):
    rows_n = f.shape[2] - 2 * MARGIN
    cols_n = f.shape[3] - 2 * MARGIN

    def at(g, dr, dc):
        return g[..., MARGIN + dr : MARGIN + dr + rows_n, MARGIN + dc : MARGIN + dc + cols_n]

    def dx(g):
        return (8.0 * (at(g, 0, 1) - at(g, 0, -1)) - (at(g, 0, 2) - at(g, 0, -2))) / 12.0

    def dy(g):
        return (8.0 * (at(g, 1, 0) - at(g, -1, 0)) - (at(g, 2, 0) - at(g, -2, 0))) / 12.0

    def lap(g):
        return at(g, 0, 1) + at(g, 0, -1) + at(g, 1, 0) + at(g, -1, 0) - 4.0 * at(g, 0, 0)

    pressure = GRAVITY * jnp.cumsum(HALINE * f[1] - THERMAL * f[0], axis=0)
    centre = at(f, 0, 0)
    east_v, north_v = centre[2], centre[3]
    advection = east_v * dx(f) + north_v * dy(f)
    mixing = jnp.array([SCALAR_MIXING, SCALAR_MIXING, VISCOSITY, VISCOSITY], jnp.float32)
    tendency = mixing.reshape(4, 1, 1, 1) * lap(f) - advection
    still = jnp.zeros_like(east_v)
    forcing = jnp.stack(
        [still, still, cor * north_v - dx(pressure), -cor * east_v - dy(pressure)]
    )
    return wet * (centre + TIME_INCREMENT * (tendency + forcing))

def shards(state, sea_mask, levels):
    n_fields, level_count, tile_rows, tile_cols = state.shape
    depth_index = jnp.arange(level_count, dtype=jnp.int32)[:, None, None]
    depth = jnp.where(sea_mask == 1, levels, 0).astype(jnp.float32)
    channels = jnp.concatenate([state.reshape(n_fields * level_count, tile_rows, tile_cols), depth[None]])
    signs = jnp.array([1.0, 1.0, -1.0, -1.0], dtype=jnp.float32)
    signs = jnp.concatenate([jnp.repeat(signs, level_count), jnp.ones((1,), jnp.float32)])
    wide_state, wide_depth = gather_wide(channels, signs[:, None, None])

    lat = lax.axis_index("lat")
    total = lax.axis_size("lat") * tile_rows
    first_row = lat * tile_rows

    grown_depth = wide_depth[MARGIN:-MARGIN, MARGIN:-MARGIN]
    grown_wet = (depth_index < grown_depth[None]).astype(jnp.float32)
    grown_rows = first_row - MARGIN + jnp.arange(tile_rows + 2 * MARGIN, dtype=jnp.int32)
    fields = wide_state.reshape(n_fields, level_count, *wide_state.shape[1:])
    once = advance(fields, grown_wet, coriolis(grown_rows, total))
    south_edge = (lat == 0) & (grown_rows < 0)
    once = jnp.where(south_edge[:, None], 0.0, once)

    wet = (depth_index < depth[None]).astype(jnp.float32)
    own_rows = first_row + jnp.arange(tile_rows, dtype=jnp.int32)
    return advance(once, wet, coriolis(own_rows, total))


def solution(mesh):
    return jax.shard_map(
        shards,
        mesh=mesh,
        in_specs=(P(None, None, "lat", "lon"), P("lat", "lon"), P("lat", "lon")),
        out_specs=P(None, None, "lat", "lon"),
        check_vma=False,
    )
```

```python
import jax
import jax.numpy as jnp
from jax import lax
from jax.sharding import PartitionSpec as P

TIME_INCREMENT = 0.1
SCALAR_MIXING = 0.4
VISCOSITY = 0.4
THERMAL = 0.2
HALINE = 0.8
GRAVITY = 0.1
MARGIN = 2
WIDE = 2 * MARGIN


def coriolis(row_index, total):
    mirrored = jnp.where(row_index >= total, 2 * total - 1 - row_index, row_index)
    return (1.2 * jnp.sin(-1.3 + 2.8 * (mirrored.astype(jnp.float32) + 0.5) / total))[:, None]


def gather_wide(x, signs):
    n_lon = lax.axis_size("lon")
    n_lat = lax.axis_size("lat")

    lat = lax.axis_index("lat")
    odd = lat % 2 == 1
    top_rows = x[:, -WIDE:, :]
    bottom_rows = x[:, :WIDE, :]
    inner = [(i, i + 1) for i in range(1, n_lat - 1, 2)]
    inner = inner + [(j, i) for i, j in inner]
    top = n_lat - 1
    pairs = [(l * n_lat + i, l * n_lat + j) for l in range(n_lon) for i, j in inner]
    pairs = pairs + [(l * n_lat + top, (n_lon - 1 - l) * n_lat + top) for l in range(n_lon)]
    to_even = lax.ppermute(jnp.where(odd, top_rows, bottom_rows), ("lon", "lat"), pairs)
    to_odd = lax.ppermute(
        jnp.where(odd, bottom_rows, top_rows),
        ("lon", "lat"),
        [(l * n_lat + i, l * n_lat + (i ^ 1)) for l in range(n_lon) for i in range(n_lat)],
    )
    folded = jnp.flip(to_even, axis=(1, 2)) * signs
    north = jnp.where(odd, jnp.where(lat == top, folded, to_even), to_odd)
    south = jnp.where(odd, to_odd, to_even)
    lat_wide = jnp.concatenate([south, x, north], axis=1)

    lon = lax.axis_index("lon")
    lon_odd = lon % 2 == 1
    edge_shape = lat_wide[..., :WIDE].shape
    east_cols = lat_wide[..., -WIDE:].reshape(-1)
    west_cols = lat_wide[..., :WIDE].reshape(-1)
    across = [(m, (m + 1) % n_lon) for m in range(1, n_lon, 2)]
    across = across + [(j, i) for i, j in across]
    off_send = jnp.where(lon_odd, east_cols, west_cols)
    off_chip = lax.ppermute(off_send, "lon", across)
    off_send, later = lax.optimization_barrier((off_send, lat_wide))
    on_send = jnp.where(lon_odd, later[..., :WIDE].reshape(-1), later[..., -WIDE:].reshape(-1))
    on_chip = lax.ppermute(on_send, "lon", [(m, m ^ 1) for m in range(n_lon)])
    west = jnp.where(lon_odd, on_chip, off_chip).reshape(edge_shape)
    east = jnp.where(lon_odd, off_chip, on_chip).reshape(edge_shape)
    wide_state = jnp.concatenate([west[:-1], lat_wide[:-1], east[:-1]], axis=2)
    wide_depth = jnp.concatenate([west[-1], lat_wide[-1], east[-1]], axis=1)
    return wide_state, wide_depth


def advance(f, wet, cor):
    rows_n = f.shape[2] - 2 * MARGIN
    cols_n = f.shape[3] - 2 * MARGIN

    def at(g, dr, dc):
        return g[..., MARGIN + dr : MARGIN + dr + rows_n, MARGIN + dc : MARGIN + dc + cols_n]

    def dx(g):
        return (8.0 * (at(g, 0, 1) - at(g, 0, -1)) - (at(g, 0, 2) - at(g, 0, -2))) / 12.0

    def dy(g):
        return (8.0 * (at(g, 1, 0) - at(g, -1, 0)) - (at(g, 2, 0) - at(g, -2, 0))) / 12.0

    def lap(g):
        return at(g, 0, 1) + at(g, 0, -1) + at(g, 1, 0) + at(g, -1, 0) - 4.0 * at(g, 0, 0)

    pressure = GRAVITY * jnp.cumsum(HALINE * f[1] - THERMAL * f[0], axis=0)
    centre = at(f, 0, 0)
    east_v, north_v = centre[2], centre[3]
    advection = east_v * dx(f) + north_v * dy(f)
    mixing = jnp.array([SCALAR_MIXING, SCALAR_MIXING, VISCOSITY, VISCOSITY], jnp.float32)
    tendency = mixing.reshape(4, 1, 1, 1) * lap(f) - advection
    still = jnp.zeros_like(east_v)
    forcing = jnp.stack(
        [still, still, cor * north_v - dx(pressure), -cor * east_v - dy(pressure)]
    )
    return wet * (centre + TIME_INCREMENT * (tendency + forcing))

def shards(state, sea_mask, levels):
    n_fields, level_count, tile_rows, tile_cols = state.shape
    depth_index = jnp.arange(level_count, dtype=jnp.int32)[:, None, None]
    depth = jnp.where(sea_mask == 1, levels, 0).astype(jnp.float32)
    channels = jnp.concatenate([state.reshape(n_fields * level_count, tile_rows, tile_cols), depth[None]])
    signs = jnp.array([1.0, 1.0, -1.0, -1.0], dtype=jnp.float32)
    signs = jnp.concatenate([jnp.repeat(signs, level_count), jnp.ones((1,), jnp.float32)])
    wide_state, wide_depth = gather_wide(channels, signs[:, None, None])

    lat = lax.axis_index("lat")
    total = lax.axis_size("lat") * tile_rows
    first_row = lat * tile_rows

    grown_depth = wide_depth[MARGIN:-MARGIN, MARGIN:-MARGIN]
    grown_wet = (depth_index < grown_depth[None]).astype(jnp.float32)
    grown_rows = first_row - MARGIN + jnp.arange(tile_rows + 2 * MARGIN, dtype=jnp.int32)
    fields = wide_state.reshape(n_fields, level_count, *wide_state.shape[1:])
    once = advance(fields, grown_wet, coriolis(grown_rows, total))
    south_edge = (lat == 0) & (grown_rows < 0)
    once = jnp.where(south_edge[:, None], 0.0, once)

    wet = (depth_index < depth[None]).astype(jnp.float32)
    own_rows = first_row + jnp.arange(tile_rows, dtype=jnp.int32)
    return advance(once, wet, coriolis(own_rows, total))


def solution(mesh):
    return jax.shard_map(
        shards,
        mesh=mesh,
        in_specs=(P(None, None, "lat", "lon"), P("lat", "lon"), P("lat", "lon")),
        out_specs=P(None, None, "lat", "lon"),
        check_vma=False,
    )
```

```python
import jax
import jax.numpy as jnp
from jax import lax
from jax.sharding import PartitionSpec as P

TIME_INCREMENT = 0.1
SCALAR_MIXING = 0.4
VISCOSITY = 0.4
THERMAL = 0.2
HALINE = 0.8
GRAVITY = 0.1
MARGIN = 2
WIDE = 2 * MARGIN


def coriolis(row_index, total):
    mirrored = jnp.where(row_index >= total, 2 * total - 1 - row_index, row_index)
    return (1.2 * jnp.sin(-1.3 + 2.8 * (mirrored.astype(jnp.float32) + 0.5) / total))[:, None]


def gather_wide(state, sea_mask, levels, signs):
    n_lon = lax.axis_size("lon")
    n_lat = lax.axis_size("lat")
    n_fields, level_count, tile_rows, tile_cols = state.shape

    def rows_of(st, mask, lev, first):
        st = st.reshape(n_fields * level_count, tile_rows, tile_cols)[:, first : first + WIDE]
        depth = jnp.where(mask[first : first + WIDE] == 1, lev[first : first + WIDE], 0)
        return jnp.concatenate([st, depth.astype(jnp.float32)[None]])

    lat = lax.axis_index("lat")
    odd = lat % 2 == 1
    top_first, bottom_first = tile_rows - WIDE, 0
    inner = [(i, i + 1) for i in range(1, n_lat - 1, 2)]
    inner = inner + [(j, i) for i, j in inner]
    top = n_lat - 1
    pairs = [(l * n_lat + i, l * n_lat + j) for l in range(n_lon) for i, j in inner]
    pairs = pairs + [(l * n_lat + top, (n_lon - 1 - l) * n_lat + top) for l in range(n_lon)]
    even_send = jnp.where(
        odd,
        rows_of(state, sea_mask, levels, top_first),
        rows_of(state, sea_mask, levels, bottom_first),
    )
    to_even = lax.ppermute(even_send, ("lon", "lat"), pairs)
    even_send, state, sea_mask, levels = lax.optimization_barrier((even_send, state, sea_mask, levels))
    odd_send = jnp.where(
        odd,
        rows_of(state, sea_mask, levels, bottom_first),
        rows_of(state, sea_mask, levels, top_first),
    )
    to_odd = lax.ppermute(
        odd_send,
        ("lon", "lat"),
        [(l * n_lat + i, l * n_lat + (i ^ 1)) for l in range(n_lon) for i in range(n_lat)],
    )
    depth = jnp.where(sea_mask == 1, levels, 0).astype(jnp.float32)
    x = jnp.concatenate([state.reshape(n_fields * level_count, tile_rows, tile_cols), depth[None]])
    folded = jnp.flip(to_even, axis=(1, 2)) * signs
    north = jnp.where(odd, jnp.where(lat == top, folded, to_even), to_odd)
    south = jnp.where(odd, to_odd, to_even)
    lat_wide = jnp.concatenate([south, x, north], axis=1)

    lon = lax.axis_index("lon")
    lon_odd = lon % 2 == 1
    edge_shape = lat_wide[..., :WIDE].shape
    east_cols = lat_wide[..., -WIDE:].reshape(-1)
    west_cols = lat_wide[..., :WIDE].reshape(-1)
    across = [(m, (m + 1) % n_lon) for m in range(1, n_lon, 2)]
    across = across + [(j, i) for i, j in across]
    off_send = jnp.where(lon_odd, east_cols, west_cols)
    off_chip = lax.ppermute(off_send, "lon", across)
    off_send, later = lax.optimization_barrier((off_send, lat_wide))
    on_send = jnp.where(lon_odd, later[..., :WIDE].reshape(-1), later[..., -WIDE:].reshape(-1))
    on_chip = lax.ppermute(on_send, "lon", [(m, m ^ 1) for m in range(n_lon)])
    west = jnp.where(lon_odd, on_chip, off_chip).reshape(edge_shape)
    east = jnp.where(lon_odd, off_chip, on_chip).reshape(edge_shape)
    wide_state = jnp.concatenate([west[:-1], lat_wide[:-1], east[:-1]], axis=2)
    wide_depth = jnp.concatenate([west[-1], lat_wide[-1], east[-1]], axis=1)
    return wide_state, wide_depth


def advance(f, wet, cor):
    rows_n = f.shape[2] - 2 * MARGIN
    cols_n = f.shape[3] - 2 * MARGIN

    def at(g, dr, dc):
        return g[..., MARGIN + dr : MARGIN + dr + rows_n, MARGIN + dc : MARGIN + dc + cols_n]

    def dx(g):
        return (8.0 * (at(g, 0, 1) - at(g, 0, -1)) - (at(g, 0, 2) - at(g, 0, -2))) / 12.0

    def dy(g):
        return (8.0 * (at(g, 1, 0) - at(g, -1, 0)) - (at(g, 2, 0) - at(g, -2, 0))) / 12.0

    def lap(g):
        return at(g, 0, 1) + at(g, 0, -1) + at(g, 1, 0) + at(g, -1, 0) - 4.0 * at(g, 0, 0)

    pressure = GRAVITY * jnp.cumsum(HALINE * f[1] - THERMAL * f[0], axis=0)
    centre = at(f, 0, 0)
    east_v, north_v = centre[2], centre[3]
    advection = east_v * dx(f) + north_v * dy(f)
    mixing = jnp.array([SCALAR_MIXING, SCALAR_MIXING, VISCOSITY, VISCOSITY], jnp.float32)
    tendency = mixing.reshape(4, 1, 1, 1) * lap(f) - advection
    still = jnp.zeros_like(east_v)
    forcing = jnp.stack(
        [still, still, cor * north_v - dx(pressure), -cor * east_v - dy(pressure)]
    )
    return wet * (centre + TIME_INCREMENT * (tendency + forcing))

def shards(state, sea_mask, levels):
    n_fields, level_count, tile_rows, tile_cols = state.shape
    depth_index = jnp.arange(level_count, dtype=jnp.int32)[:, None, None]
    depth = jnp.where(sea_mask == 1, levels, 0).astype(jnp.float32)
    signs = jnp.array([1.0, 1.0, -1.0, -1.0], dtype=jnp.float32)
    signs = jnp.concatenate([jnp.repeat(signs, level_count), jnp.ones((1,), jnp.float32)])
    wide_state, wide_depth = gather_wide(state, sea_mask, levels, signs[:, None, None])

    lat = lax.axis_index("lat")
    total = lax.axis_size("lat") * tile_rows
    first_row = lat * tile_rows

    grown_depth = wide_depth[MARGIN:-MARGIN, MARGIN:-MARGIN]
    grown_wet = (depth_index < grown_depth[None]).astype(jnp.float32)
    grown_rows = first_row - MARGIN + jnp.arange(tile_rows + 2 * MARGIN, dtype=jnp.int32)
    fields = wide_state.reshape(n_fields, level_count, *wide_state.shape[1:])
    once = advance(fields, grown_wet, coriolis(grown_rows, total))
    south_edge = (lat == 0) & (grown_rows < 0)
    once = jnp.where(south_edge[:, None], 0.0, once)

    wet = (depth_index < depth[None]).astype(jnp.float32)
    own_rows = first_row + jnp.arange(tile_rows, dtype=jnp.int32)
    return advance(once, wet, coriolis(own_rows, total))


def solution(mesh):
    return jax.shard_map(
        shards,
        mesh=mesh,
        in_specs=(P(None, None, "lat", "lon"), P("lat", "lon"), P("lat", "lon")),
        out_specs=P(None, None, "lat", "lon"),
        check_vma=False,
    )
```

```python
import jax
import jax.numpy as jnp
from jax import lax
from jax.sharding import PartitionSpec as P

TIME_INCREMENT = 0.1
SCALAR_MIXING = 0.4
VISCOSITY = 0.4
THERMAL = 0.2
HALINE = 0.8
GRAVITY = 0.1
MARGIN = 2
WIDE = 2 * MARGIN


def coriolis(row_index, total):
    mirrored = jnp.where(row_index >= total, 2 * total - 1 - row_index, row_index)
    return (1.2 * jnp.sin(-1.3 + 2.8 * (mirrored.astype(jnp.float32) + 0.5) / total))[:, None]


def gather_wide(state, sea_mask, levels, signs):
    n_lon = lax.axis_size("lon")
    n_lat = lax.axis_size("lat")
    n_fields, level_count, tile_rows, tile_cols = state.shape

    def rows_of(st, mask, lev, first):
        st = st.reshape(n_fields * level_count, tile_rows, tile_cols)[:, first : first + WIDE]
        depth = jnp.where(mask[first : first + WIDE] == 1, lev[first : first + WIDE], 0)
        return jnp.concatenate([st, depth.astype(jnp.float32)[None]])

    lat = lax.axis_index("lat")
    odd = lat % 2 == 1
    top_first, bottom_first = tile_rows - WIDE, 0
    inner = [(i, i + 1) for i in range(1, n_lat - 1, 2)]
    inner = inner + [(j, i) for i, j in inner]
    top = n_lat - 1
    pairs = [(l * n_lat + i, l * n_lat + j) for l in range(n_lon) for i, j in inner]
    pairs = pairs + [(l * n_lat + top, (n_lon - 1 - l) * n_lat + top) for l in range(n_lon)]
    odd_send = jnp.where(
        odd,
        rows_of(state, sea_mask, levels, bottom_first),
        rows_of(state, sea_mask, levels, top_first),
    )
    to_odd = lax.ppermute(
        odd_send,
        ("lon", "lat"),
        [(l * n_lat + i, l * n_lat + (i ^ 1)) for l in range(n_lon) for i in range(n_lat)],
    )
    odd_send, state, sea_mask, levels = lax.optimization_barrier((odd_send, state, sea_mask, levels))
    even_send = jnp.where(
        odd,
        rows_of(state, sea_mask, levels, top_first),
        rows_of(state, sea_mask, levels, bottom_first),
    )
    to_even = lax.ppermute(even_send, ("lon", "lat"), pairs)
    depth = jnp.where(sea_mask == 1, levels, 0).astype(jnp.float32)
    x = jnp.concatenate([state.reshape(n_fields * level_count, tile_rows, tile_cols), depth[None]])
    folded = jnp.flip(to_even, axis=(1, 2)) * signs
    north = jnp.where(odd, jnp.where(lat == top, folded, to_even), to_odd)
    south = jnp.where(odd, to_odd, to_even)
    lat_wide = jnp.concatenate([south, x, north], axis=1)

    lon = lax.axis_index("lon")
    lon_odd = lon % 2 == 1
    edge_shape = lat_wide[..., :WIDE].shape
    east_cols = lat_wide[..., -WIDE:].reshape(-1)
    west_cols = lat_wide[..., :WIDE].reshape(-1)
    across = [(m, (m + 1) % n_lon) for m in range(1, n_lon, 2)]
    across = across + [(j, i) for i, j in across]
    off_send = jnp.where(lon_odd, east_cols, west_cols)
    off_chip = lax.ppermute(off_send, "lon", across)
    off_send, later = lax.optimization_barrier((off_send, lat_wide))
    on_send = jnp.where(lon_odd, later[..., :WIDE].reshape(-1), later[..., -WIDE:].reshape(-1))
    on_chip = lax.ppermute(on_send, "lon", [(m, m ^ 1) for m in range(n_lon)])
    west = jnp.where(lon_odd, on_chip, off_chip).reshape(edge_shape)
    east = jnp.where(lon_odd, off_chip, on_chip).reshape(edge_shape)
    wide_state = jnp.concatenate([west[:-1], lat_wide[:-1], east[:-1]], axis=2)
    wide_depth = jnp.concatenate([west[-1], lat_wide[-1], east[-1]], axis=1)
    return wide_state, wide_depth


def advance(f, wet, cor):
    rows_n = f.shape[2] - 2 * MARGIN
    cols_n = f.shape[3] - 2 * MARGIN

    def at(g, dr, dc):
        return g[..., MARGIN + dr : MARGIN + dr + rows_n, MARGIN + dc : MARGIN + dc + cols_n]

    def dx(g):
        return (8.0 * (at(g, 0, 1) - at(g, 0, -1)) - (at(g, 0, 2) - at(g, 0, -2))) / 12.0

    def dy(g):
        return (8.0 * (at(g, 1, 0) - at(g, -1, 0)) - (at(g, 2, 0) - at(g, -2, 0))) / 12.0

    def lap(g):
        return at(g, 0, 1) + at(g, 0, -1) + at(g, 1, 0) + at(g, -1, 0) - 4.0 * at(g, 0, 0)

    pressure = GRAVITY * jnp.cumsum(HALINE * f[1] - THERMAL * f[0], axis=0)
    centre = at(f, 0, 0)
    east_v, north_v = centre[2], centre[3]
    advection = east_v * dx(f) + north_v * dy(f)
    mixing = jnp.array([SCALAR_MIXING, SCALAR_MIXING, VISCOSITY, VISCOSITY], jnp.float32)
    tendency = mixing.reshape(4, 1, 1, 1) * lap(f) - advection
    still = jnp.zeros_like(east_v)
    forcing = jnp.stack(
        [still, still, cor * north_v - dx(pressure), -cor * east_v - dy(pressure)]
    )
    return wet * (centre + TIME_INCREMENT * (tendency + forcing))

def shards(state, sea_mask, levels):
    n_fields, level_count, tile_rows, tile_cols = state.shape
    depth_index = jnp.arange(level_count, dtype=jnp.int32)[:, None, None]
    depth = jnp.where(sea_mask == 1, levels, 0).astype(jnp.float32)
    signs = jnp.array([1.0, 1.0, -1.0, -1.0], dtype=jnp.float32)
    signs = jnp.concatenate([jnp.repeat(signs, level_count), jnp.ones((1,), jnp.float32)])
    wide_state, wide_depth = gather_wide(state, sea_mask, levels, signs[:, None, None])

    lat = lax.axis_index("lat")
    total = lax.axis_size("lat") * tile_rows
    first_row = lat * tile_rows

    grown_depth = wide_depth[MARGIN:-MARGIN, MARGIN:-MARGIN]
    grown_wet = (depth_index < grown_depth[None]).astype(jnp.float32)
    grown_rows = first_row - MARGIN + jnp.arange(tile_rows + 2 * MARGIN, dtype=jnp.int32)
    fields = wide_state.reshape(n_fields, level_count, *wide_state.shape[1:])
    once = advance(fields, grown_wet, coriolis(grown_rows, total))
    south_edge = (lat == 0) & (grown_rows < 0)
    once = jnp.where(south_edge[:, None], 0.0, once)

    wet = (depth_index < depth[None]).astype(jnp.float32)
    own_rows = first_row + jnp.arange(tile_rows, dtype=jnp.int32)
    return advance(once, wet, coriolis(own_rows, total))


def solution(mesh):
    return jax.shard_map(
        shards,
        mesh=mesh,
        in_specs=(P(None, None, "lat", "lon"), P("lat", "lon"), P("lat", "lon")),
        out_specs=P(None, None, "lat", "lon"),
        check_vma=False,
    )
```

```python
import jax
import jax.numpy as jnp
from jax import lax
from jax.sharding import PartitionSpec as P

TIME_INCREMENT = 0.1
SCALAR_MIXING = 0.4
VISCOSITY = 0.4
THERMAL = 0.2
HALINE = 0.8
GRAVITY = 0.1
MARGIN = 2
WIDE = 2 * MARGIN


def coriolis(row_index, total):
    mirrored = jnp.where(row_index >= total, 2 * total - 1 - row_index, row_index)
    return (1.2 * jnp.sin(-1.3 + 2.8 * (mirrored.astype(jnp.float32) + 0.5) / total))[:, None]


def gather_wide(x, signs):
    n_lon = lax.axis_size("lon")
    n_lat = lax.axis_size("lat")

    lat = lax.axis_index("lat")
    odd = lat % 2 == 1
    top_rows = x[:, -WIDE:, :]
    bottom_rows = x[:, :WIDE, :]
    inner = [(i, i + 1) for i in range(1, n_lat - 1, 2)]
    inner = inner + [(j, i) for i, j in inner]
    top = n_lat - 1
    pairs = [(l * n_lat + i, l * n_lat + j) for l in range(n_lon) for i, j in inner]
    pairs = pairs + [(l * n_lat + top, (n_lon - 1 - l) * n_lat + top) for l in range(n_lon)]
    to_even = lax.ppermute(jnp.where(odd, top_rows, bottom_rows), ("lon", "lat"), pairs)
    to_odd = lax.ppermute(
        jnp.where(odd, bottom_rows, top_rows),
        ("lon", "lat"),
        [(l * n_lat + i, l * n_lat + (i ^ 1)) for l in range(n_lon) for i in range(n_lat)],
    )
    folded = jnp.flip(to_even, axis=(1, 2)) * signs
    north = jnp.where(odd, jnp.where(lat == top, folded, to_even), to_odd)
    south = jnp.where(odd, to_odd, to_even)
    lat_wide = jnp.concatenate([south, x, north], axis=1)

    lon = lax.axis_index("lon")
    lon_odd = lon % 2 == 1
    edge_shape = lat_wide[..., :WIDE].shape
    east_cols = lat_wide[..., -WIDE:].reshape(-1)
    west_cols = lat_wide[..., :WIDE].reshape(-1)
    across = [(m, (m + 1) % n_lon) for m in range(1, n_lon, 2)]
    across = across + [(j, i) for i, j in across]
    off_send = jnp.where(lon_odd, east_cols, west_cols)
    off_chip = lax.ppermute(off_send, "lon", across)
    off_send, later = lax.optimization_barrier((off_send, lat_wide))
    on_send = jnp.where(lon_odd, later[..., :WIDE].reshape(-1), later[..., -WIDE:].reshape(-1))
    on_chip = lax.ppermute(on_send, "lon", [(m, m ^ 1) for m in range(n_lon)])
    near = on_chip.reshape(edge_shape)
    far = off_chip.reshape(edge_shape)
    wide_state = jnp.where(
        lon_odd,
        jnp.concatenate([near[:-1], lat_wide[:-1], far[:-1]], axis=2),
        jnp.concatenate([far[:-1], lat_wide[:-1], near[:-1]], axis=2),
    )
    wide_depth = jnp.where(
        lon_odd,
        jnp.concatenate([near[-1], lat_wide[-1], far[-1]], axis=1),
        jnp.concatenate([far[-1], lat_wide[-1], near[-1]], axis=1),
    )
    return wide_state, wide_depth


def advance(f, wet, cor):
    rows_n = f.shape[2] - 2 * MARGIN
    cols_n = f.shape[3] - 2 * MARGIN

    def at(g, dr, dc):
        return g[..., MARGIN + dr : MARGIN + dr + rows_n, MARGIN + dc : MARGIN + dc + cols_n]

    def dx(g):
        return (8.0 * (at(g, 0, 1) - at(g, 0, -1)) - (at(g, 0, 2) - at(g, 0, -2))) / 12.0

    def dy(g):
        return (8.0 * (at(g, 1, 0) - at(g, -1, 0)) - (at(g, 2, 0) - at(g, -2, 0))) / 12.0

    def lap(g):
        return at(g, 0, 1) + at(g, 0, -1) + at(g, 1, 0) + at(g, -1, 0) - 4.0 * at(g, 0, 0)

    pressure = GRAVITY * jnp.cumsum(HALINE * f[1] - THERMAL * f[0], axis=0)
    centre = at(f, 0, 0)
    east_v, north_v = centre[2], centre[3]
    advection = east_v * dx(f) + north_v * dy(f)
    mixing = jnp.array([SCALAR_MIXING, SCALAR_MIXING, VISCOSITY, VISCOSITY], jnp.float32)
    tendency = mixing.reshape(4, 1, 1, 1) * lap(f) - advection
    still = jnp.zeros_like(east_v)
    forcing = jnp.stack(
        [still, still, cor * north_v - dx(pressure), -cor * east_v - dy(pressure)]
    )
    return wet * (centre + TIME_INCREMENT * (tendency + forcing))

def shards(state, sea_mask, levels):
    n_fields, level_count, tile_rows, tile_cols = state.shape
    depth_index = jnp.arange(level_count, dtype=jnp.int32)[:, None, None]
    depth = jnp.where(sea_mask == 1, levels, 0).astype(jnp.float32)
    channels = jnp.concatenate([state.reshape(n_fields * level_count, tile_rows, tile_cols), depth[None]])
    signs = jnp.array([1.0, 1.0, -1.0, -1.0], dtype=jnp.float32)
    signs = jnp.concatenate([jnp.repeat(signs, level_count), jnp.ones((1,), jnp.float32)])
    wide_state, wide_depth = gather_wide(channels, signs[:, None, None])

    lat = lax.axis_index("lat")
    total = lax.axis_size("lat") * tile_rows
    first_row = lat * tile_rows

    grown_depth = wide_depth[MARGIN:-MARGIN, MARGIN:-MARGIN]
    grown_wet = (depth_index < grown_depth[None]).astype(jnp.float32)
    grown_rows = first_row - MARGIN + jnp.arange(tile_rows + 2 * MARGIN, dtype=jnp.int32)
    fields = wide_state.reshape(n_fields, level_count, *wide_state.shape[1:])
    once = advance(fields, grown_wet, coriolis(grown_rows, total))
    south_edge = (lat == 0) & (grown_rows < 0)
    once = jnp.where(south_edge[:, None], 0.0, once)

    wet = (depth_index < depth[None]).astype(jnp.float32)
    own_rows = first_row + jnp.arange(tile_rows, dtype=jnp.int32)
    return advance(once, wet, coriolis(own_rows, total))


def solution(mesh):
    return jax.shard_map(
        shards,
        mesh=mesh,
        in_specs=(P(None, None, "lat", "lon"), P("lat", "lon"), P("lat", "lon")),
        out_specs=P(None, None, "lat", "lon"),
        check_vma=False,
    )
```

```python
import jax
import jax.numpy as jnp
from jax import lax
from jax.sharding import PartitionSpec as P

TIME_INCREMENT = 0.1
SCALAR_MIXING = 0.4
VISCOSITY = 0.4
THERMAL = 0.2
HALINE = 0.8
GRAVITY = 0.1
MARGIN = 2
WIDE = 2 * MARGIN


def coriolis(row_index, total):
    mirrored = jnp.where(row_index >= total, 2 * total - 1 - row_index, row_index)
    return (1.2 * jnp.sin(-1.3 + 2.8 * (mirrored.astype(jnp.float32) + 0.5) / total))[:, None]


def gather_wide(x, signs):
    n_lon = lax.axis_size("lon")
    n_lat = lax.axis_size("lat")

    lat = lax.axis_index("lat")
    odd = lat % 2 == 1
    top_rows = x[:, -WIDE:, :]
    bottom_rows = x[:, :WIDE, :]
    inner = [(i, i + 1) for i in range(1, n_lat - 1, 2)]
    inner = inner + [(j, i) for i, j in inner]
    top = n_lat - 1
    pairs = [(l * n_lat + i, l * n_lat + j) for l in range(n_lon) for i, j in inner]
    pairs = pairs + [(l * n_lat + top, (n_lon - 1 - l) * n_lat + top) for l in range(n_lon)]
    to_even = lax.ppermute(jnp.where(odd, top_rows, bottom_rows), ("lon", "lat"), pairs)
    to_odd = lax.ppermute(
        jnp.where(odd, bottom_rows, top_rows),
        ("lon", "lat"),
        [(l * n_lat + i, l * n_lat + (i ^ 1)) for l in range(n_lon) for i in range(n_lat)],
    )
    folded = jnp.flip(to_even, axis=(1, 2)) * signs
    north = jnp.where(odd, jnp.where(lat == top, folded, to_even), to_odd)
    south = jnp.where(odd, to_odd, to_even)
    lat_wide = jnp.concatenate([south, x, north], axis=1)

    lon = lax.axis_index("lon")
    lon_odd = lon % 2 == 1
    used = lat_wide[:, MARGIN:-MARGIN]
    edge_shape = used[..., :WIDE].shape
    east_cols = used[..., -WIDE:].reshape(-1)
    west_cols = used[..., :WIDE].reshape(-1)
    across = [(m, (m + 1) % n_lon) for m in range(1, n_lon, 2)]
    across = across + [(j, i) for i, j in across]
    off_send = jnp.where(lon_odd, east_cols, west_cols)
    off_chip = lax.ppermute(off_send, "lon", across)
    off_send, later = lax.optimization_barrier((off_send, lat_wide))
    later = later[:, MARGIN:-MARGIN]
    on_send = jnp.where(lon_odd, later[..., :WIDE].reshape(-1), later[..., -WIDE:].reshape(-1))
    on_chip = lax.ppermute(on_send, "lon", [(m, m ^ 1) for m in range(n_lon)])
    rim = ((0, 0), (MARGIN, MARGIN), (0, 0))
    west = jnp.pad(jnp.where(lon_odd, on_chip, off_chip).reshape(edge_shape), rim)
    east = jnp.pad(jnp.where(lon_odd, off_chip, on_chip).reshape(edge_shape), rim)
    wide_state = jnp.concatenate([west[:-1], lat_wide[:-1], east[:-1]], axis=2)
    wide_depth = jnp.concatenate([west[-1], lat_wide[-1], east[-1]], axis=1)
    return wide_state, wide_depth


def advance(f, wet, cor):
    rows_n = f.shape[2] - 2 * MARGIN
    cols_n = f.shape[3] - 2 * MARGIN

    def at(g, dr, dc):
        return g[..., MARGIN + dr : MARGIN + dr + rows_n, MARGIN + dc : MARGIN + dc + cols_n]

    def dx(g):
        return (8.0 * (at(g, 0, 1) - at(g, 0, -1)) - (at(g, 0, 2) - at(g, 0, -2))) / 12.0

    def dy(g):
        return (8.0 * (at(g, 1, 0) - at(g, -1, 0)) - (at(g, 2, 0) - at(g, -2, 0))) / 12.0

    def lap(g):
        return at(g, 0, 1) + at(g, 0, -1) + at(g, 1, 0) + at(g, -1, 0) - 4.0 * at(g, 0, 0)

    pressure = GRAVITY * jnp.cumsum(HALINE * f[1] - THERMAL * f[0], axis=0)
    centre = at(f, 0, 0)
    east_v, north_v = centre[2], centre[3]
    advection = east_v * dx(f) + north_v * dy(f)
    mixing = jnp.array([SCALAR_MIXING, SCALAR_MIXING, VISCOSITY, VISCOSITY], jnp.float32)
    tendency = mixing.reshape(4, 1, 1, 1) * lap(f) - advection
    still = jnp.zeros_like(east_v)
    forcing = jnp.stack(
        [still, still, cor * north_v - dx(pressure), -cor * east_v - dy(pressure)]
    )
    return wet * (centre + TIME_INCREMENT * (tendency + forcing))

def shards(state, sea_mask, levels):
    n_fields, level_count, tile_rows, tile_cols = state.shape
    depth_index = jnp.arange(level_count, dtype=jnp.int32)[:, None, None]
    depth = jnp.where(sea_mask == 1, levels, 0).astype(jnp.float32)
    channels = jnp.concatenate([state.reshape(n_fields * level_count, tile_rows, tile_cols), depth[None]])
    signs = jnp.array([1.0, 1.0, -1.0, -1.0], dtype=jnp.float32)
    signs = jnp.concatenate([jnp.repeat(signs, level_count), jnp.ones((1,), jnp.float32)])
    wide_state, wide_depth = gather_wide(channels, signs[:, None, None])

    lat = lax.axis_index("lat")
    total = lax.axis_size("lat") * tile_rows
    first_row = lat * tile_rows

    grown_depth = wide_depth[MARGIN:-MARGIN, MARGIN:-MARGIN]
    grown_wet = (depth_index < grown_depth[None]).astype(jnp.float32)
    grown_rows = first_row - MARGIN + jnp.arange(tile_rows + 2 * MARGIN, dtype=jnp.int32)
    fields = wide_state.reshape(n_fields, level_count, *wide_state.shape[1:])
    once = advance(fields, grown_wet, coriolis(grown_rows, total))
    south_edge = (lat == 0) & (grown_rows < 0)
    once = jnp.where(south_edge[:, None], 0.0, once)

    wet = (depth_index < depth[None]).astype(jnp.float32)
    own_rows = first_row + jnp.arange(tile_rows, dtype=jnp.int32)
    return advance(once, wet, coriolis(own_rows, total))


def solution(mesh):
    return jax.shard_map(
        shards,
        mesh=mesh,
        in_specs=(P(None, None, "lat", "lon"), P("lat", "lon"), P("lat", "lon")),
        out_specs=P(None, None, "lat", "lon"),
        check_vma=False,
    )
```

```python
import jax
import jax.numpy as jnp
from jax import lax
from jax.sharding import PartitionSpec as P

TIME_INCREMENT = 0.1
SCALAR_MIXING = 0.4
VISCOSITY = 0.4
THERMAL = 0.2
HALINE = 0.8
GRAVITY = 0.1
MARGIN = 2
WIDE = 2 * MARGIN


def coriolis(row_index, total):
    mirrored = jnp.where(row_index >= total, 2 * total - 1 - row_index, row_index)
    return (1.2 * jnp.sin(-1.3 + 2.8 * (mirrored.astype(jnp.float32) + 0.5) / total))[:, None]


def gather_wide(x, signs):
    n_lon = lax.axis_size("lon")
    n_lat = lax.axis_size("lat")

    lat = lax.axis_index("lat")
    odd = lat % 2 == 1
    top_rows = x[:, -WIDE:, :]
    bottom_rows = x[:, :WIDE, :]
    inner = [(i, i + 1) for i in range(1, n_lat - 1, 2)]
    inner = inner + [(j, i) for i, j in inner]
    top = n_lat - 1
    pairs = [(l * n_lat + i, l * n_lat + j) for l in range(n_lon) for i, j in inner]
    pairs = pairs + [(l * n_lat + top, (n_lon - 1 - l) * n_lat + top) for l in range(n_lon)]
    to_even = lax.ppermute(jnp.where(odd, top_rows, bottom_rows), ("lon", "lat"), pairs)
    to_odd = lax.ppermute(
        jnp.where(odd, bottom_rows, top_rows),
        ("lon", "lat"),
        [(l * n_lat + i, l * n_lat + (i ^ 1)) for l in range(n_lon) for i in range(n_lat)],
    )
    folded = jnp.flip(to_even, axis=(1, 2)) * signs
    north = jnp.where(odd, jnp.where(lat == top, folded, to_even), to_odd)
    south = jnp.where(odd, to_odd, to_even)
    lat_wide = jnp.concatenate([south, x, north], axis=1)

    lon = lax.axis_index("lon")
    lon_odd = lon % 2 == 1
    used = lat_wide[:, MARGIN:-MARGIN]
    edge_shape = used[..., :WIDE].shape
    east_cols = used[..., -WIDE:].reshape(-1)
    west_cols = used[..., :WIDE].reshape(-1)
    across = [(m, (m + 1) % n_lon) for m in range(1, n_lon, 2)]
    across = across + [(j, i) for i, j in across]
    off_send = jnp.where(lon_odd, east_cols, west_cols)
    off_chip = lax.ppermute(off_send, "lon", across)
    off_send, later = lax.optimization_barrier((off_send, lat_wide))
    later = later[:, MARGIN:-MARGIN]
    on_send = jnp.where(lon_odd, later[..., :WIDE].reshape(-1), later[..., -WIDE:].reshape(-1))
    on_chip = lax.ppermute(on_send, "lon", [(m, m ^ 1) for m in range(n_lon)])
    rim = ((0, 0), (MARGIN, MARGIN), (0, 0))
    west = jnp.pad(jnp.where(lon_odd, on_chip, off_chip).reshape(edge_shape), rim)
    east = jnp.pad(jnp.where(lon_odd, off_chip, on_chip).reshape(edge_shape), rim)
    lat_state = jnp.concatenate([south[:-1], x[:-1], north[:-1]], axis=1)
    lat_depth = jnp.concatenate([south[-1], x[-1], north[-1]], axis=0)
    wide_state = jnp.concatenate([west[:-1], lat_state, east[:-1]], axis=2)
    wide_depth = jnp.concatenate([west[-1], lat_depth, east[-1]], axis=1)
    return wide_state, wide_depth


def advance(f, wet, cor):
    rows_n = f.shape[2] - 2 * MARGIN
    cols_n = f.shape[3] - 2 * MARGIN

    def at(g, dr, dc):
        return g[..., MARGIN + dr : MARGIN + dr + rows_n, MARGIN + dc : MARGIN + dc + cols_n]

    def dx(g):
        return (8.0 * (at(g, 0, 1) - at(g, 0, -1)) - (at(g, 0, 2) - at(g, 0, -2))) / 12.0

    def dy(g):
        return (8.0 * (at(g, 1, 0) - at(g, -1, 0)) - (at(g, 2, 0) - at(g, -2, 0))) / 12.0

    def lap(g):
        return at(g, 0, 1) + at(g, 0, -1) + at(g, 1, 0) + at(g, -1, 0) - 4.0 * at(g, 0, 0)

    pressure = GRAVITY * jnp.cumsum(HALINE * f[1] - THERMAL * f[0], axis=0)
    centre = at(f, 0, 0)
    east_v, north_v = centre[2], centre[3]
    advection = east_v * dx(f) + north_v * dy(f)
    mixing = jnp.array([SCALAR_MIXING, SCALAR_MIXING, VISCOSITY, VISCOSITY], jnp.float32)
    tendency = mixing.reshape(4, 1, 1, 1) * lap(f) - advection
    still = jnp.zeros_like(east_v)
    forcing = jnp.stack(
        [still, still, cor * north_v - dx(pressure), -cor * east_v - dy(pressure)]
    )
    return wet * (centre + TIME_INCREMENT * (tendency + forcing))

def shards(state, sea_mask, levels):
    n_fields, level_count, tile_rows, tile_cols = state.shape
    depth_index = jnp.arange(level_count, dtype=jnp.int32)[:, None, None]
    depth = jnp.where(sea_mask == 1, levels, 0).astype(jnp.float32)
    channels = jnp.concatenate([state.reshape(n_fields * level_count, tile_rows, tile_cols), depth[None]])
    signs = jnp.array([1.0, 1.0, -1.0, -1.0], dtype=jnp.float32)
    signs = jnp.concatenate([jnp.repeat(signs, level_count), jnp.ones((1,), jnp.float32)])
    wide_state, wide_depth = gather_wide(channels, signs[:, None, None])

    lat = lax.axis_index("lat")
    total = lax.axis_size("lat") * tile_rows
    first_row = lat * tile_rows

    grown_depth = wide_depth[MARGIN:-MARGIN, MARGIN:-MARGIN]
    grown_wet = (depth_index < grown_depth[None]).astype(jnp.float32)
    grown_rows = first_row - MARGIN + jnp.arange(tile_rows + 2 * MARGIN, dtype=jnp.int32)
    fields = wide_state.reshape(n_fields, level_count, *wide_state.shape[1:])
    once = advance(fields, grown_wet, coriolis(grown_rows, total))
    south_edge = (lat == 0) & (grown_rows < 0)
    once = jnp.where(south_edge[:, None], 0.0, once)

    wet = (depth_index < depth[None]).astype(jnp.float32)
    own_rows = first_row + jnp.arange(tile_rows, dtype=jnp.int32)
    return advance(once, wet, coriolis(own_rows, total))


def solution(mesh):
    return jax.shard_map(
        shards,
        mesh=mesh,
        in_specs=(P(None, None, "lat", "lon"), P("lat", "lon"), P("lat", "lon")),
        out_specs=P(None, None, "lat", "lon"),
        check_vma=False,
    )
```

```python
import jax
import jax.numpy as jnp
from jax import lax
from jax.sharding import PartitionSpec as P

TIME_INCREMENT = 0.1
SCALAR_MIXING = 0.4
VISCOSITY = 0.4
THERMAL = 0.2
HALINE = 0.8
GRAVITY = 0.1
MARGIN = 2
WIDE = 2 * MARGIN


def coriolis(row_index, total):
    mirrored = jnp.where(row_index >= total, 2 * total - 1 - row_index, row_index)
    return (1.2 * jnp.sin(-1.3 + 2.8 * (mirrored.astype(jnp.float32) + 0.5) / total))[:, None]


def gather_wide(x, signs):
    n_lon = lax.axis_size("lon")
    n_lat = lax.axis_size("lat")

    lat = lax.axis_index("lat")
    odd = lat % 2 == 1
    top_rows = x[:, -WIDE:, :]
    bottom_rows = x[:, :WIDE, :]
    inner = [(i, i + 1) for i in range(1, n_lat - 1, 2)]
    inner = inner + [(j, i) for i, j in inner]
    top = n_lat - 1
    pairs = [(l * n_lat + i, l * n_lat + j) for l in range(n_lon) for i, j in inner]
    pairs = pairs + [(l * n_lat + top, (n_lon - 1 - l) * n_lat + top) for l in range(n_lon)]
    to_even = lax.ppermute(jnp.where(odd, top_rows, bottom_rows), ("lon", "lat"), pairs)
    to_odd = lax.ppermute(
        jnp.where(odd, bottom_rows, top_rows),
        ("lon", "lat"),
        [(l * n_lat + i, l * n_lat + (i ^ 1)) for l in range(n_lon) for i in range(n_lat)],
    )
    folded = jnp.flip(to_even, axis=(1, 2)) * signs
    north = jnp.where(odd, jnp.where(lat == top, folded, to_even), to_odd)
    south = jnp.where(odd, to_odd, to_even)
    lat_wide = jnp.concatenate([south, x, north], axis=1)

    lon = lax.axis_index("lon")
    lon_odd = lon % 2 == 1
    used = lat_wide[:, MARGIN:-MARGIN]
    edge_shape = used[..., :WIDE].shape
    east_cols = used[..., -WIDE:].reshape(-1)
    west_cols = used[..., :WIDE].reshape(-1)
    across = [(m, (m + 1) % n_lon) for m in range(1, n_lon, 2)]
    across = across + [(j, i) for i, j in across]
    off_send = jnp.where(lon_odd, east_cols, west_cols)
    off_chip = lax.ppermute(off_send, "lon", across)
    off_send, later, south, x, north = lax.optimization_barrier((off_send, lat_wide, south, x, north))
    later = later[:, MARGIN:-MARGIN]
    on_send = jnp.where(lon_odd, later[..., :WIDE].reshape(-1), later[..., -WIDE:].reshape(-1))
    on_chip = lax.ppermute(on_send, "lon", [(m, m ^ 1) for m in range(n_lon)])
    rim = ((0, 0), (MARGIN, MARGIN), (0, 0))
    west = jnp.pad(jnp.where(lon_odd, on_chip, off_chip).reshape(edge_shape), rim)
    east = jnp.pad(jnp.where(lon_odd, off_chip, on_chip).reshape(edge_shape), rim)
    lat_state = jnp.concatenate([south[:-1], x[:-1], north[:-1]], axis=1)
    lat_depth = jnp.concatenate([south[-1], x[-1], north[-1]], axis=0)
    wide_state = jnp.pad(lat_state, ((0, 0), (0, 0), (WIDE, WIDE)))
    wide_state = lax.dynamic_update_slice(wide_state, west[:-1], (0, 0, 0))
    wide_state = lax.dynamic_update_slice(wide_state, east[:-1], (0, 0, wide_state.shape[2] - WIDE))
    wide_depth = jnp.concatenate([west[-1], lat_depth, east[-1]], axis=1)
    return wide_state, wide_depth


def advance(f, wet, cor):
    rows_n = f.shape[2] - 2 * MARGIN
    cols_n = f.shape[3] - 2 * MARGIN

    def at(g, dr, dc):
        return g[..., MARGIN + dr : MARGIN + dr + rows_n, MARGIN + dc : MARGIN + dc + cols_n]

    def dx(g):
        return (8.0 * (at(g, 0, 1) - at(g, 0, -1)) - (at(g, 0, 2) - at(g, 0, -2))) / 12.0

    def dy(g):
        return (8.0 * (at(g, 1, 0) - at(g, -1, 0)) - (at(g, 2, 0) - at(g, -2, 0))) / 12.0

    def lap(g):
        return at(g, 0, 1) + at(g, 0, -1) + at(g, 1, 0) + at(g, -1, 0) - 4.0 * at(g, 0, 0)

    pressure = GRAVITY * jnp.cumsum(HALINE * f[1] - THERMAL * f[0], axis=0)
    centre = at(f, 0, 0)
    east_v, north_v = centre[2], centre[3]
    advection = east_v * dx(f) + north_v * dy(f)
    mixing = jnp.array([SCALAR_MIXING, SCALAR_MIXING, VISCOSITY, VISCOSITY], jnp.float32)
    tendency = mixing.reshape(4, 1, 1, 1) * lap(f) - advection
    still = jnp.zeros_like(east_v)
    forcing = jnp.stack(
        [still, still, cor * north_v - dx(pressure), -cor * east_v - dy(pressure)]
    )
    return wet * (centre + TIME_INCREMENT * (tendency + forcing))

def shards(state, sea_mask, levels):
    n_fields, level_count, tile_rows, tile_cols = state.shape
    depth_index = jnp.arange(level_count, dtype=jnp.int32)[:, None, None]
    depth = jnp.where(sea_mask == 1, levels, 0).astype(jnp.float32)
    channels = jnp.concatenate([state.reshape(n_fields * level_count, tile_rows, tile_cols), depth[None]])
    signs = jnp.array([1.0, 1.0, -1.0, -1.0], dtype=jnp.float32)
    signs = jnp.concatenate([jnp.repeat(signs, level_count), jnp.ones((1,), jnp.float32)])
    wide_state, wide_depth = gather_wide(channels, signs[:, None, None])

    lat = lax.axis_index("lat")
    total = lax.axis_size("lat") * tile_rows
    first_row = lat * tile_rows

    grown_depth = wide_depth[MARGIN:-MARGIN, MARGIN:-MARGIN]
    grown_wet = (depth_index < grown_depth[None]).astype(jnp.float32)
    grown_rows = first_row - MARGIN + jnp.arange(tile_rows + 2 * MARGIN, dtype=jnp.int32)
    fields = wide_state.reshape(n_fields, level_count, *wide_state.shape[1:])
    once = advance(fields, grown_wet, coriolis(grown_rows, total))
    south_edge = (lat == 0) & (grown_rows < 0)
    once = jnp.where(south_edge[:, None], 0.0, once)

    wet = (depth_index < depth[None]).astype(jnp.float32)
    own_rows = first_row + jnp.arange(tile_rows, dtype=jnp.int32)
    return advance(once, wet, coriolis(own_rows, total))


def solution(mesh):
    return jax.shard_map(
        shards,
        mesh=mesh,
        in_specs=(P(None, None, "lat", "lon"), P("lat", "lon"), P("lat", "lon")),
        out_specs=P(None, None, "lat", "lon"),
        check_vma=False,
    )
```

```python
import jax
import jax.numpy as jnp
from jax import lax
from jax.sharding import PartitionSpec as P

TIME_INCREMENT = 0.1
SCALAR_MIXING = 0.4
VISCOSITY = 0.4
THERMAL = 0.2
HALINE = 0.8
GRAVITY = 0.1
MARGIN = 2
WIDE = 2 * MARGIN


def coriolis(row_index, total):
    mirrored = jnp.where(row_index >= total, 2 * total - 1 - row_index, row_index)
    return (1.2 * jnp.sin(-1.3 + 2.8 * (mirrored.astype(jnp.float32) + 0.5) / total))[:, None]


def gather_wide(x, signs, edge_rows):
    n_lon = lax.axis_size("lon")
    n_lat = lax.axis_size("lat")

    lat = lax.axis_index("lat")
    odd = lat % 2 == 1
    top_rows, bottom_rows = edge_rows
    inner = [(i, i + 1) for i in range(1, n_lat - 1, 2)]
    inner = inner + [(j, i) for i, j in inner]
    top = n_lat - 1
    pairs = [(l * n_lat + i, l * n_lat + j) for l in range(n_lon) for i, j in inner]
    pairs = pairs + [(l * n_lat + top, (n_lon - 1 - l) * n_lat + top) for l in range(n_lon)]
    to_even = lax.ppermute(jnp.where(odd, top_rows, bottom_rows), ("lon", "lat"), pairs)
    to_odd = lax.ppermute(
        jnp.where(odd, bottom_rows, top_rows),
        ("lon", "lat"),
        [(l * n_lat + i, l * n_lat + (i ^ 1)) for l in range(n_lon) for i in range(n_lat)],
    )
    folded = jnp.flip(to_even, axis=(1, 2)) * signs
    north = jnp.where(odd, jnp.where(lat == top, folded, to_even), to_odd)
    south = jnp.where(odd, to_odd, to_even)
    lat_wide = jnp.concatenate([south, x, north], axis=1)

    lon = lax.axis_index("lon")
    lon_odd = lon % 2 == 1
    used = lat_wide[:, MARGIN:-MARGIN]
    edge_shape = used[..., :WIDE].shape
    east_cols = used[..., -WIDE:].reshape(-1)
    west_cols = used[..., :WIDE].reshape(-1)
    across = [(m, (m + 1) % n_lon) for m in range(1, n_lon, 2)]
    across = across + [(j, i) for i, j in across]
    off_send = jnp.where(lon_odd, east_cols, west_cols)
    off_chip = lax.ppermute(off_send, "lon", across)
    off_send, later = lax.optimization_barrier((off_send, lat_wide))
    later = later[:, MARGIN:-MARGIN]
    on_send = jnp.where(lon_odd, later[..., :WIDE].reshape(-1), later[..., -WIDE:].reshape(-1))
    on_chip = lax.ppermute(on_send, "lon", [(m, m ^ 1) for m in range(n_lon)])
    rim = ((0, 0), (MARGIN, MARGIN), (0, 0))
    west = jnp.pad(jnp.where(lon_odd, on_chip, off_chip).reshape(edge_shape), rim)
    east = jnp.pad(jnp.where(lon_odd, off_chip, on_chip).reshape(edge_shape), rim)
    lat_state = jnp.concatenate([south[:-1], x[:-1], north[:-1]], axis=1)
    lat_depth = jnp.concatenate([south[-1], x[-1], north[-1]], axis=0)
    wide_state = jnp.concatenate([west[:-1], lat_state, east[:-1]], axis=2)
    wide_depth = jnp.concatenate([west[-1], lat_depth, east[-1]], axis=1)
    return wide_state, wide_depth


def advance(f, wet, cor):
    rows_n = f.shape[2] - 2 * MARGIN
    cols_n = f.shape[3] - 2 * MARGIN

    def at(g, dr, dc):
        return g[..., MARGIN + dr : MARGIN + dr + rows_n, MARGIN + dc : MARGIN + dc + cols_n]

    def dx(g):
        return (8.0 * (at(g, 0, 1) - at(g, 0, -1)) - (at(g, 0, 2) - at(g, 0, -2))) / 12.0

    def dy(g):
        return (8.0 * (at(g, 1, 0) - at(g, -1, 0)) - (at(g, 2, 0) - at(g, -2, 0))) / 12.0

    def lap(g):
        return at(g, 0, 1) + at(g, 0, -1) + at(g, 1, 0) + at(g, -1, 0) - 4.0 * at(g, 0, 0)

    pressure = GRAVITY * jnp.cumsum(HALINE * f[1] - THERMAL * f[0], axis=0)
    centre = at(f, 0, 0)
    east_v, north_v = centre[2], centre[3]
    advection = east_v * dx(f) + north_v * dy(f)
    mixing = jnp.array([SCALAR_MIXING, SCALAR_MIXING, VISCOSITY, VISCOSITY], jnp.float32)
    tendency = mixing.reshape(4, 1, 1, 1) * lap(f) - advection
    still = jnp.zeros_like(east_v)
    forcing = jnp.stack(
        [still, still, cor * north_v - dx(pressure), -cor * east_v - dy(pressure)]
    )
    return wet * (centre + TIME_INCREMENT * (tendency + forcing))

def shards(state, sea_mask, levels):
    n_fields, level_count, tile_rows, tile_cols = state.shape
    depth_index = jnp.arange(level_count, dtype=jnp.int32)[:, None, None]
    depth = jnp.where(sea_mask == 1, levels, 0).astype(jnp.float32)
    channels = jnp.concatenate([state.reshape(n_fields * level_count, tile_rows, tile_cols), depth[None]])
    signs = jnp.array([1.0, 1.0, -1.0, -1.0], dtype=jnp.float32)
    signs = jnp.concatenate([jnp.repeat(signs, level_count), jnp.ones((1,), jnp.float32)])
    def edge(first):
        rows = slice(first, first + WIDE)
        own = state.reshape(n_fields * level_count, tile_rows, tile_cols)[:, rows]
        deep = jnp.where(sea_mask[rows] == 1, levels[rows], 0).astype(jnp.float32)
        return jnp.concatenate([own, deep[None]])

    edge_rows = (edge(tile_rows - WIDE), edge(0))
    wide_state, wide_depth = gather_wide(channels, signs[:, None, None], edge_rows)

    lat = lax.axis_index("lat")
    total = lax.axis_size("lat") * tile_rows
    first_row = lat * tile_rows

    grown_depth = wide_depth[MARGIN:-MARGIN, MARGIN:-MARGIN]
    grown_wet = (depth_index < grown_depth[None]).astype(jnp.float32)
    grown_rows = first_row - MARGIN + jnp.arange(tile_rows + 2 * MARGIN, dtype=jnp.int32)
    fields = wide_state.reshape(n_fields, level_count, *wide_state.shape[1:])
    once = advance(fields, grown_wet, coriolis(grown_rows, total))
    south_edge = (lat == 0) & (grown_rows < 0)
    once = jnp.where(south_edge[:, None], 0.0, once)

    wet = (depth_index < depth[None]).astype(jnp.float32)
    own_rows = first_row + jnp.arange(tile_rows, dtype=jnp.int32)
    return advance(once, wet, coriolis(own_rows, total))


def solution(mesh):
    return jax.shard_map(
        shards,
        mesh=mesh,
        in_specs=(P(None, None, "lat", "lon"), P("lat", "lon"), P("lat", "lon")),
        out_specs=P(None, None, "lat", "lon"),
        check_vma=False,
    )
```
